32 devices in a mesh: dp: 16 (over z, y, x), mp: 2 (over core).
Axes of the slice: x: 2, y: 2, z: 4, core: 2. Of those that a mesh axis runs over, the one named last changes fastest.
Arguments:
- tokens: bfloat16 [7168, 4544], P('dp'), may hold values from -32 to 32
- layer_norm_gain: bfloat16 [4544], replicated, may hold values from 0.5 to 1.5
- layer_norm_bias: bfloat16 [4544], replicated, may hold values from -3 to 3
- query_weight: bfloat16 [4544, 4096], P('dp', 'mp'), may hold values from -3 to 3
- key_value_weight: bfloat16 [4544, 128], P('dp'), may hold values from -3 to 3
- output_weight: bfloat16 [4096, 4544], P('dp', 'mp'), may hold values from -0.09375 to 0.09375
- adapter_down_factors: bfloat16 [16, 4544, 16], P('dp', 'mp'), may hold values from -0.09375 to 0.09375
- adapter_up_factors: bfloat16 [16, 16, 4096], P('dp', None, 'mp'), may hold values from -1.5 to 1.5
- lengths: int32 [16, 4], P('dp'), may hold values from 1 to 224, 448 in all within a row
- prompt_adapter: int32 [16, 4], P('dp'), may hold values from 0 to 15
- prompt_page_table: int32 [16, 8], P('dp'), may hold values from 0 to 7, each once within a row
- adapter_storage: int32 [16], replicated, may hold values from 0 to 15, each once
Outputs:
- attn_proj: bfloat16 [7168, 4544], P('dp', 'mp')
- kv_cache: bfloat16 [128, 128, 128], P('dp')
The draws below stay inside these ranges and needn't reach their ends.
Inputs may be any that keep to these rules, and one draw needn't show every extreme that they name: `lengths`: each row sums to 448. `prompt_page_table`: row r lists each of the 8 pages of the pool of dp index r once; entry p * 2 + k is the page of tokens k * 128 to (k + 1) * 128 - 1 of that row's prompt p. `adapter_storage`: every storage slot holds exactly one adapter.
All inputs are finite; a program needn't handle non-finite values.
Results may differ from the reference program's by a relative error of at most 0.012.
The reference program's roundings to bfloat16 on the way (of `normed`, `ranks`, `queries`, `kv_rot`, `probs` and `context`) count: a program that leaves them out, or rounds other values in their place, can miss the bound.
Values may be sent and summed in bfloat16 or wider, within the bound.
No kernel may reach another device: no remote copies, remote signals or barrier semaphores. Data moves between devices by JAX's collectives and lax.ppermute only.
A program may use at most 192 MiB of HBM per device.

```python
import math
import jax
import jax.numpy as jnp
import numpy as np
from jax import lax

MODEL_WIDTH = 4544
HEAD_SIZE = 64
QUERY_HEADS = 64
ADAPTER_RANK = 16
PAGE = 128
P_DEV = 4
TOK_DEV = 448
LMAX = 224
PAGES_DEV = 8
ADAPTER_TOTAL = 16
TOKENS = 7168
N_DP = 16


def drawn_weight(key, salt, rows, cols):
    values = jax.random.normal(jax.random.fold_in(key, salt), (rows, cols), jnp.float32)
    return jnp.clip(values, -6.0, 6.0) * (1.0 / math.sqrt(rows))


def draw_tokens(key, part):
    values = jax.random.normal(jax.random.fold_in(key, 9203), (TOKENS, MODEL_WIDTH), jnp.float32)
    return jnp.clip(values, -6.0, 6.0).astype(jnp.bfloat16)


def draw_key_value_weight(key, part):
    return drawn_weight(key, 9201, MODEL_WIDTH, 2 * HEAD_SIZE).astype(jnp.bfloat16)


def draw_query_weight(key, part):
    return drawn_weight(key, 9202, MODEL_WIDTH, QUERY_HEADS * HEAD_SIZE).astype(jnp.bfloat16)


def with_ends(values, key, low, largest):
    dims = values.shape
    place = [jax.random.randint(jax.random.fold_in(key, axis), (), 0, dims[axis]) for axis in range(len(dims))]
    values = values.at[tuple(place)].set(low)
    longest = dims.index(max(dims))
    place[longest] = (place[longest] + 1) % dims[longest]
    return values.at[tuple(place)].set(largest)


def block_scale(key, shape, shards, smallest, top_value):
    factor_of, own = 1.0, jax.random.fold_in(key, 6)
    for dim, blocks in shards:
        heights = jnp.exp(jax.random.uniform(jax.random.fold_in(own, dim), (blocks,), jnp.float32, smallest / len(shards), top_value / len(shards)))
        factor_of = factor_of * jnp.repeat(heights, shape[dim] // blocks).reshape([-1 if axis == dim else 1 for axis in range(len(shape))])
    return factor_of


def cumulative_ranks(count, lean):
    loads = [(1 << 20) // math.isqrt(standing ** lean) + 1 for standing in range(1, count + 1)]
    deviation = 1 + sum(loads) // (1 << 30)
    return np.cumsum(np.array([max(1, weight // deviation) for weight in loads]))


def ranked(own_key, extent, number_of, skew):
    grid = cumulative_ranks(number_of, skew)
    pick = jax.random.randint(jax.random.fold_in(own_key, 1), extent, 0, int(grid[number_of - 1]))
    rank = jnp.searchsorted(jnp.asarray(grid, jnp.int32), pick, side="right")
    return jax.random.permutation(jax.random.fold_in(own_key, 2), number_of)[rank].astype(jnp.int32)


def profile(amount, total, reach, skew):
    portions = [(1 << 20) // math.isqrt(grade ** skew) + 1 for grade in range(2, amount + 1)]
    surplus, holding = total - reach - (amount - 1), [1] * (amount - 1)
    while surplus > 0:
        movable = [i for i in range(amount - 1) if holding[i] < reach]
        pool, budget = sum([portions[i] for i in movable]), surplus
        for i in movable:
            extra = min(reach - holding[i], max(1, budget * portions[i] // pool), surplus)
            holding[i] = holding[i] + extra
            surplus = surplus - extra
    return np.array([reach] + holding)


def ragged_sizes(own_key, amount, total, limit, lean):
    if amount == 2:
        one = jax.random.randint(own_key, (), max(1, total - limit), min(limit, total - 1) + 1)
        return jnp.stack([one, total - one])
    tallies = jnp.asarray(profile(amount, total, limit, lean), jnp.int32)
    pairs = (amount - 1) // 2
    donor, receiver = tallies[1:1 + 2 * pairs:2], tallies[2:2 + 2 * pairs:2]
    room = jnp.minimum(donor - 1, limit - receiver)
    moved = jax.random.randint(jax.random.fold_in(own_key, 1), (pairs,), 0, 1 << 20) % (room + 1)
    tallies = tallies.at[1:1 + 2 * pairs:2].set(donor - moved).at[2:2 + 2 * pairs:2].set(receiver + moved)
    return tallies[jax.random.permutation(jax.random.fold_in(own_key, 2), amount)]


def normal_values(key, shape, deviation, reach, pieces=(), held_as=jnp.bfloat16):
    values = jax.random.normal(key, shape, jnp.float32) * deviation
    if len(pieces) > 0:
        values = block_scale(key, shape, pieces, -0.22, 0.18) * values
    return jnp.clip(values, min=-reach, max=reach).astype(held_as)


def setup_inputs(seed: int = 0) -> dict:
    key_of = jax.random.split(jax.random.key(seed), 13)
    return {
        "tokens": draw_tokens(jax.random.fold_in(key_of[12], 71), 0),
        "layer_norm_gain": jnp.clip(1.0 + 0.1 * jax.random.normal(key_of[1], (MODEL_WIDTH,), jnp.float32), 0.5, 1.5).astype(jnp.bfloat16),
        "layer_norm_bias": normal_values(key_of[2], (MODEL_WIDTH,), 0.5, 3.0),
        "query_weight": draw_query_weight(jax.random.fold_in(key_of[12], 71), 0),
        "key_value_weight": draw_key_value_weight(jax.random.fold_in(key_of[12], 71), 0),
        "output_weight": normal_values(key_of[5], (QUERY_HEADS * HEAD_SIZE, MODEL_WIDTH), (QUERY_HEADS * HEAD_SIZE) ** -0.5, 0.09375, ((0, 16), (1, 2))),
        "adapter_down_factors": normal_values(key_of[6], (ADAPTER_TOTAL, MODEL_WIDTH, ADAPTER_RANK), MODEL_WIDTH ** -0.5, 0.09375, ((0, 16), (1, 2))),
        "adapter_up_factors": normal_values(key_of[7], (ADAPTER_TOTAL, ADAPTER_RANK, QUERY_HEADS * HEAD_SIZE), ADAPTER_RANK ** -0.5, 1.5, ((0, 16), (2, 2))),
        "lengths": jax.vmap(lambda own: ragged_sizes(own, P_DEV, TOK_DEV, LMAX, 2))(jax.random.split(key_of[8], N_DP)).reshape((N_DP, P_DEV)).astype(jnp.int32),
        "prompt_adapter": with_ends(ranked(key_of[9], (N_DP, P_DEV), ADAPTER_TOTAL, 2), jax.random.fold_in(key_of[9], 3), 0, ADAPTER_TOTAL - 1).astype(jnp.int32),
        "prompt_page_table": jax.vmap(lambda own: jax.random.permutation(own, PAGES_DEV))(jax.random.split(key_of[10], N_DP)).reshape((N_DP, PAGES_DEV)).astype(jnp.int32),
        "adapter_storage": jax.random.permutation(key_of[11], ADAPTER_TOTAL).astype(jnp.int32),
    }


def layer_norm(tokens, layer_norm_gain, layer_norm_bias):
    values = tokens.astype(jnp.float32)
    row_mean = lax.optimization_barrier(jnp.mean(values, axis=-1, keepdims=True))
    centred = values - row_mean
    row_var = lax.optimization_barrier(jnp.mean(centred * centred, axis=-1, keepdims=True))
    scaled = centred * lax.rsqrt(row_var + 1e-05)
    return (scaled * layer_norm_gain.astype(jnp.float32) + layer_norm_bias.astype(jnp.float32)).astype(jnp.bfloat16)

def layout(lengths_row, row_number_count):
    prompt_end = jnp.cumsum(lengths_row).astype(jnp.int32)
    prompt_start = (prompt_end - lengths_row).astype(jnp.int32)
    row_index = jnp.arange(row_number_count, dtype=jnp.int32)
    member = (row_index[:, None] >= prompt_start[None, :]) & (row_index[:, None] < prompt_end[None, :])
    first_row = lax.optimization_barrier(jnp.sum(jnp.where(member, prompt_start[None, :], 0), axis=1)).astype(jnp.int32)
    prompt_numbers = jnp.arange(lengths_row.shape[0], dtype=jnp.int32)
    prompt_index = lax.optimization_barrier(jnp.sum(jnp.where(member, prompt_numbers[None, :], 0), axis=1)).astype(jnp.int32)
    position = (row_index - first_row).astype(jnp.float32)
    return (member, position, prompt_start, prompt_index)

def rotate(values, position):
    half_width = values.shape[-1] // 2
    frequency = jnp.exp(jnp.arange(half_width, dtype=jnp.float32) * (-math.log(10000.0) / half_width))
    angles = position[:, None, None] * frequency[None, None, :]
    cosine = jnp.cos(angles)
    sine = jnp.sin(angles)
    leading = values[..., :half_width]
    trailing = values[..., half_width:]
    return jnp.concatenate([leading * cosine - trailing * sine, trailing * cosine + leading * sine], axis=-1)

def attend(queries, keys_rot, values, prompt_index):
    row_number_count = queries.shape[0]
    head_width = queries.shape[2]
    row_index = jnp.arange(row_number_count, dtype=jnp.int32)
    allowed = (prompt_index[:, None] == prompt_index[None, :]) & (row_index[None, :] <= row_index[:, None])
    scores = jnp.einsum('thd,sd->hts', queries.astype(jnp.float32), keys_rot.astype(jnp.float32)) * (1.0 / math.sqrt(head_width))
    scores = jnp.where(allowed[None, :, :], scores, -jnp.inf)
    row_peak = lax.optimization_barrier(jnp.max(scores, axis=-1, keepdims=True))
    weights = jnp.exp(scores - row_peak)
    probs = (weights / lax.optimization_barrier(jnp.sum(weights, axis=-1, keepdims=True))).astype(jnp.bfloat16)
    context = jnp.einsum('hts,sd->thd', probs.astype(jnp.float32), values.astype(jnp.float32))
    return context.astype(jnp.bfloat16)

def fill_pages(kv_rot, lengths_row, prompt_start, table_row, page_slots):
    page_count = table_row.shape[0]
    prompt_count = lengths_row.shape[0]
    per_prompt = page_count // prompt_count
    page_index = jnp.arange(page_count, dtype=jnp.int32)
    entry = lax.optimization_barrier(jnp.sum(jnp.where(table_row[None, :] == page_index[:, None], page_index[None, :], 0), axis=1)).astype(jnp.int32)
    prompt_of = entry // per_prompt
    page_of = entry % per_prompt
    prompt_numbers = jnp.arange(prompt_count, dtype=jnp.int32)
    chosen = prompt_of[:, None] == prompt_numbers[None, :]
    prompt_len = lax.optimization_barrier(jnp.sum(jnp.where(chosen, lengths_row[None, :], 0), axis=1)).astype(jnp.int32)
    base_row = lax.optimization_barrier(jnp.sum(jnp.where(chosen, prompt_start[None, :], 0), axis=1)).astype(jnp.int32)
    within = page_of[:, None] * page_slots + jnp.arange(page_slots, dtype=jnp.int32)[None, :]
    valid = within < prompt_len[:, None]
    source = jnp.minimum(base_row[:, None] + within, kv_rot.shape[0] - 1).astype(jnp.int32)
    return jnp.where(valid[:, :, None], kv_rot[source], jnp.zeros((), kv_rot.dtype))

def single_group(input_rows, layer_norm_gain, layer_norm_bias, query_weight, key_value_weight, output_weight, adapter_down_factors, adapter_up_factors, adapter_storage):
    tokens, lengths_row, adapters_row, table_row = input_rows
    row_number_count = tokens.shape[0]
    member, position, prompt_start, prompt_index = layout(lengths_row, row_number_count)
    normed = layer_norm(tokens, layer_norm_gain, layer_norm_bias)
    storage_slots = adapter_storage[adapters_row]
    down_selected = adapter_down_factors[storage_slots]
    up_selected = adapter_up_factors[storage_slots]
    member_weight = member.astype(jnp.float32)
    rank_sum = jnp.zeros((row_number_count, ADAPTER_RANK), jnp.float32)
    for prompt in range(P_DEV):
        rank_sum = rank_sum + member_weight[:, prompt:prompt + 1] * jnp.dot(normed, down_selected[prompt], preferred_element_type=jnp.float32)
    ranks = rank_sum.astype(jnp.bfloat16)
    adapted_queries = jnp.zeros((row_number_count, QUERY_HEADS * HEAD_SIZE), jnp.float32)
    for prompt in range(P_DEV):
        adapted_queries = adapted_queries + member_weight[:, prompt:prompt + 1] * jnp.dot(ranks, up_selected[prompt], preferred_element_type=jnp.float32)
    query_sum = jnp.dot(normed, query_weight, preferred_element_type=jnp.float32) + adapted_queries
    queries = rotate(query_sum.reshape(row_number_count, QUERY_HEADS, HEAD_SIZE), position).astype(jnp.bfloat16)
    kv_base = jnp.dot(normed, key_value_weight, preferred_element_type=jnp.float32)
    keys_rot = rotate(kv_base[:, None, :HEAD_SIZE], position)[:, 0, :]
    kv_rot = jnp.concatenate([keys_rot, kv_base[:, HEAD_SIZE:]], axis=1).astype(jnp.bfloat16)
    context = attend(queries, kv_rot[:, :HEAD_SIZE], kv_rot[:, HEAD_SIZE:], prompt_index).reshape(row_number_count, QUERY_HEADS * HEAD_SIZE)
    attn_proj = jnp.dot(context, output_weight, preferred_element_type=jnp.float32).astype(jnp.bfloat16)
    cache = fill_pages(kv_rot, lengths_row, prompt_start, table_row, PAGE)
    return (attn_proj, cache)

def reference(tokens, layer_norm_gain, layer_norm_bias, query_weight, key_value_weight, output_weight, adapter_down_factors, adapter_up_factors, lengths, prompt_adapter, prompt_page_table, adapter_storage):
    grouped = tokens.reshape(N_DP, TOK_DEV, MODEL_WIDTH)

    def run_group(input_rows):
        return single_group(input_rows, layer_norm_gain, layer_norm_bias, query_weight, key_value_weight, output_weight, adapter_down_factors, adapter_up_factors, adapter_storage)
    outputs, caches = lax.map(run_group, (grouped, lengths, prompt_adapter, prompt_page_table))
    return (outputs.reshape(TOKENS, MODEL_WIDTH), caches.reshape(N_DP * PAGES_DEV, PAGE, 2 * HEAD_SIZE))
```

```python
import math

import jax
import jax.numpy as jnp
from jax import lax
from jax.sharding import PartitionSpec as P
from jax.experimental.layout import Layout, with_layout_constraint

HEAD_SIZE = 64
PAGE = 128


def pack_columns(part, shard_rows):
    flat = part.reshape(-1)
    width = -(-flat.shape[0] // shard_rows)
    flat = jnp.pad(flat, (0, width * shard_rows - flat.shape[0]))
    return flat.reshape(shard_rows, width)


def unpack_columns(block, shape):
    shard_count = block.shape[0]
    size = math.prod(shape)
    flat = block.reshape(shard_count, -1)[:, :size]
    return flat.reshape((shard_count * shape[0],) + tuple(shape[1:]))


def row_major(x):
    return with_layout_constraint(x, Layout(major_to_minor=tuple(range(x.ndim))))


def layer_norm(tokens, layer_norm_gain, layer_norm_bias):
    values = tokens.astype(jnp.float32)
    row_mean = jnp.mean(values, axis=-1, keepdims=True)
    centred = values - row_mean
    row_var = jnp.mean(centred * centred, axis=-1, keepdims=True)
    scaled = centred * lax.rsqrt(row_var + 1e-05)
    return (
        scaled * layer_norm_gain.astype(jnp.float32) + layer_norm_bias.astype(jnp.float32)
    ).astype(jnp.bfloat16)


def layout(lengths_row, row_number_count):
    prompt_end = jnp.cumsum(lengths_row)
    prompt_start = prompt_end - lengths_row
    row_index = jnp.arange(row_number_count, dtype=jnp.int32)
    member = (row_index[:, None] >= prompt_start[None, :]) & (
        row_index[:, None] < prompt_end[None, :]
    )
    first_row = jnp.sum(jnp.where(member, prompt_start[None, :], 0), axis=1)
    prompt_numbers = jnp.arange(lengths_row.shape[0], dtype=jnp.int32)
    prompt_index = jnp.sum(jnp.where(member, prompt_numbers[None, :], 0), axis=1)
    position = (row_index - first_row).astype(jnp.float32)
    return (member, position, prompt_start, prompt_index)


def rotate(values, position):
    half_width = values.shape[-1] // 2
    frequency = jnp.exp(
        jnp.arange(half_width, dtype=jnp.float32) * (-math.log(10000.0) / half_width)
    )
    angles = position[:, None, None] * frequency[None, None, :]
    cosine = jnp.cos(angles)
    sine = jnp.sin(angles)
    leading = values[..., :half_width]
    trailing = values[..., half_width:]
    return jnp.concatenate(
        [leading * cosine - trailing * sine, trailing * cosine + leading * sine], axis=-1
    )


def attend(queries, keys_rot, values, prompt_index):
    row_number_count = queries.shape[0]
    head_width = queries.shape[2]
    row_index = jnp.arange(row_number_count, dtype=jnp.int32)
    allowed = (prompt_index[:, None] == prompt_index[None, :]) & (
        row_index[None, :] <= row_index[:, None]
    )
    scores = jnp.einsum("thd,sd->hts", queries, keys_rot, preferred_element_type=jnp.float32) * (
        1.0 / math.sqrt(head_width)
    )
    scores = jnp.where(allowed[None, :, :], scores, -jnp.inf)
    row_peak = jnp.max(scores, axis=-1, keepdims=True)
    weights = jnp.exp(scores - row_peak)
    probs = (weights / jnp.sum(weights, axis=-1, keepdims=True)).astype(jnp.bfloat16)
    context = jnp.einsum("hts,sd->thd", probs, values, preferred_element_type=jnp.float32)
    return context.astype(jnp.bfloat16)


def fill_pages(kv_rot, lengths_row, prompt_start, table_row, page_slots):
    page_count = table_row.shape[0]
    prompt_count = lengths_row.shape[0]
    per_prompt = page_count // prompt_count
    page_index = jnp.arange(page_count, dtype=jnp.int32)
    entry = jnp.sum(
        jnp.where(table_row[None, :] == page_index[:, None], page_index[None, :], 0), axis=1
    )
    prompt_of = entry // per_prompt
    page_of = entry % per_prompt
    prompt_numbers = jnp.arange(prompt_count, dtype=jnp.int32)
    chosen = prompt_of[:, None] == prompt_numbers[None, :]
    prompt_len = jnp.sum(jnp.where(chosen, lengths_row[None, :], 0), axis=1)
    base_row = jnp.sum(jnp.where(chosen, prompt_start[None, :], 0), axis=1)
    within = page_of[:, None] * page_slots + jnp.arange(page_slots, dtype=jnp.int32)[None, :]
    valid = within < prompt_len[:, None]
    source = jnp.minimum(base_row[:, None] + within, kv_rot.shape[0] - 1)
    return jnp.where(valid[:, :, None], kv_rot[source], jnp.zeros((), kv_rot.dtype))


def shards(
    tokens,
    layer_norm_gain,
    layer_norm_bias,
    query_weight,
    key_value_weight,
    output_weight,
    adapter_down_factors,
    adapter_up_factors,
    lengths,
    prompt_adapter,
    prompt_page_table,
    adapter_storage,
):
    row_number_count = tokens.shape[0]
    group_count = lengths.shape[0]
    group_rows = row_number_count // group_count
    prompt_count = lengths.shape[1]
    total_prompts = group_count * prompt_count
    member_grouped, position_grouped, start_grouped, index_grouped = jax.vmap(
        lambda one_row: layout(one_row, group_rows)
    )(lengths)
    position = position_grouped.reshape(row_number_count)
    prompt_global = (
        index_grouped + (jnp.arange(group_count, dtype=jnp.int32) * prompt_count)[:, None]
    ).reshape(row_number_count)
    member_weight = (
        prompt_global[:, None] == jnp.arange(total_prompts, dtype=jnp.int32)[None, :]
    ).astype(jnp.float32)
    normed = layer_norm(tokens, layer_norm_gain, layer_norm_bias)

    def add_rows(piece):
        return jnp.dot(normed, piece, preferred_element_type=jnp.float32)

    shard_rows = query_weight.shape[0]
    packed_parts = (query_weight, key_value_weight, adapter_down_factors, adapter_up_factors)
    packed_cols = [pack_columns(part, shard_rows) for part in packed_parts]
    widths = [part.shape[1] for part in packed_cols]
    gathered = lax.all_gather(jnp.concatenate(packed_cols, axis=1), "dp", axis=0, tiled=False)
    offsets = [sum(widths[:i]) for i in range(len(widths))]
    unpacked = [
        unpack_columns(gathered[:, :, off : off + width], part.shape)
        for off, width, part in zip(offsets, widths, packed_parts)
    ]
    query_base = add_rows(unpacked[0])
    kv_base = add_rows(unpacked[1])
    adapters_flat = prompt_adapter.reshape(total_prompts)
    adapter_count = adapter_storage.shape[0]
    adapter_numbers = jnp.arange(adapter_count, dtype=jnp.int32)
    storage_slots = jnp.sum(
        jnp.where(adapter_numbers[None, :] == adapters_flat[:, None], adapter_storage[None, :], 0),
        axis=1,
    )
    pieces = (unpacked[2], unpacked[3])
    piece_rows = pieces[0].shape[0]
    matches = (storage_slots[:, None] == jnp.arange(piece_rows, dtype=jnp.int32)[None, :]).astype(
        jnp.bfloat16
    )
    down_part = jnp.einsum("pn,ndr->pdr", matches, pieces[0], preferred_element_type=jnp.float32)
    up_part = jnp.einsum("pn,nrc->prc", matches, pieces[1], preferred_element_type=jnp.float32)
    down_selected = down_part.astype(jnp.bfloat16)
    up_selected = up_part.astype(jnp.bfloat16)
    feature_columns = adapter_down_factors.shape[1]
    features = lax.dynamic_slice_in_dim(
        normed, lax.axis_index("mp") * feature_columns, feature_columns, 1
    )
    rank_portion = jnp.zeros((row_number_count, adapter_down_factors.shape[2]), jnp.float32)
    for prompt in range(total_prompts):
        rank_portion = rank_portion + member_weight[:, prompt : prompt + 1] * jnp.dot(
            features, down_selected[prompt], preferred_element_type=jnp.float32
        )
    ranks = lax.psum(rank_portion, "mp").astype(jnp.bfloat16)
    adapted_queries = jnp.zeros((row_number_count, adapter_up_factors.shape[2]), jnp.float32)
    for prompt in range(total_prompts):
        adapted_queries = adapted_queries + member_weight[:, prompt : prompt + 1] * jnp.dot(
            ranks, up_selected[prompt], preferred_element_type=jnp.float32
        )
    queries = rotate(
        (query_base + adapted_queries).reshape(row_number_count, -1, HEAD_SIZE), position
    ).astype(jnp.bfloat16)
    keys_rot = rotate(kv_base[:, None, :HEAD_SIZE], position)[:, 0, :]
    kv_rot = jnp.concatenate([keys_rot, kv_base[:, HEAD_SIZE:]], axis=1).astype(jnp.bfloat16)
    local_heads = queries.shape[1]
    queries_grouped = queries.reshape(group_count, group_rows, local_heads, HEAD_SIZE)
    kv_grouped = kv_rot.reshape(group_count, group_rows, 2 * HEAD_SIZE)
    context_grouped = jax.vmap(
        lambda q_part, kv_part, idx_part: attend(
            q_part, kv_part[:, :HEAD_SIZE], kv_part[:, HEAD_SIZE:], idx_part
        )
    )(queries_grouped, kv_grouped, index_grouped)
    context = context_grouped.reshape(row_number_count, local_heads * HEAD_SIZE)
    context_all = lax.all_gather(context, "mp", axis=1, tiled=True)
    projected = jnp.dot(
        context_all,
        row_major(lax.all_gather(output_weight, "dp", axis=0, tiled=True)),
        preferred_element_type=jnp.float32,
    )
    attn_proj = projected.astype(jnp.bfloat16)
    cache_grouped = jax.vmap(
        lambda kv_part, len_part, start_part, table_part: fill_pages(
            kv_part, len_part, start_part, table_part, PAGE
        )
    )(kv_grouped, lengths, start_grouped, prompt_page_table)
    kv_cache = cache_grouped.reshape(group_count * prompt_page_table.shape[1], PAGE, 2 * HEAD_SIZE)
    return (attn_proj, kv_cache)


def solution(mesh):
    return jax.shard_map(
        shards,
        mesh=mesh,
        in_specs=(
            P("dp", None),
            P(),
            P(),
            P("dp", "mp"),
            P("dp", None),
            P("dp", "mp"),
            P("dp", "mp", None),
            P("dp", None, "mp"),
            P("dp", None),
            P("dp", None),
            P("dp", None),
            P(),
        ),
        out_specs=(P("dp", "mp"), P("dp", None, None)),
        check_vma=False,
    )
```

```python
import functools
import math

import jax
import jax.numpy as jnp
from jax import lax
from jax.sharding import Mesh, PartitionSpec as P
from jax.experimental.layout import Layout, with_layout_constraint

HEAD_SIZE = 64
PAGE = 128


def pack_columns(part, shard_rows):
    flat = part.reshape(-1)
    width = -(-flat.shape[0] // shard_rows)
    flat = jnp.pad(flat, (0, width * shard_rows - flat.shape[0]))
    return flat.reshape(shard_rows, width)


def unpack_columns(block, shape):
    shard_count = block.shape[0]
    size = math.prod(shape)
    flat = block.reshape(shard_count, -1)[:, :size]
    return flat.reshape((shard_count * shape[0],) + tuple(shape[1:]))


def row_major(x):
    return with_layout_constraint(x, Layout(major_to_minor=tuple(range(x.ndim))))


def layer_norm(tokens, layer_norm_gain, layer_norm_bias):
    values = tokens.astype(jnp.float32)
    row_mean = jnp.mean(values, axis=-1, keepdims=True)
    centred = values - row_mean
    row_var = jnp.mean(centred * centred, axis=-1, keepdims=True)
    scaled = centred * lax.rsqrt(row_var + 1e-05)
    return (
        scaled * layer_norm_gain.astype(jnp.float32) + layer_norm_bias.astype(jnp.float32)
    ).astype(jnp.bfloat16)


def layout(lengths_row, row_number_count):
    prompt_end = jnp.cumsum(lengths_row)
    prompt_start = prompt_end - lengths_row
    row_index = jnp.arange(row_number_count, dtype=jnp.int32)
    member = (row_index[:, None] >= prompt_start[None, :]) & (
        row_index[:, None] < prompt_end[None, :]
    )
    first_row = jnp.sum(jnp.where(member, prompt_start[None, :], 0), axis=1)
    prompt_numbers = jnp.arange(lengths_row.shape[0], dtype=jnp.int32)
    prompt_index = jnp.sum(jnp.where(member, prompt_numbers[None, :], 0), axis=1)
    position = (row_index - first_row).astype(jnp.float32)
    return (member, position, prompt_start, prompt_index)


def rotate(values, position):
    half_width = values.shape[-1] // 2
    frequency = jnp.exp(
        jnp.arange(half_width, dtype=jnp.float32) * (-math.log(10000.0) / half_width)
    )
    angles = position[:, None, None] * frequency[None, None, :]
    cosine = jnp.cos(angles)
    sine = jnp.sin(angles)
    leading = values[..., :half_width]
    trailing = values[..., half_width:]
    return jnp.concatenate(
        [leading * cosine - trailing * sine, trailing * cosine + leading * sine], axis=-1
    )


def attend(queries, keys_rot, values, prompt_index):
    row_number_count = queries.shape[0]
    head_width = queries.shape[2]
    row_index = jnp.arange(row_number_count, dtype=jnp.int32)
    allowed = (prompt_index[:, None] == prompt_index[None, :]) & (
        row_index[None, :] <= row_index[:, None]
    )
    scores = jnp.einsum("thd,sd->hts", queries, keys_rot, preferred_element_type=jnp.float32) * (
        1.0 / math.sqrt(head_width)
    )
    scores = jnp.where(allowed[None, :, :], scores, -jnp.inf)
    row_peak = jnp.max(scores, axis=-1, keepdims=True)
    weights = jnp.exp(scores - row_peak)
    probs = (weights / jnp.sum(weights, axis=-1, keepdims=True)).astype(jnp.bfloat16)
    context = jnp.einsum("hts,sd->thd", probs, values, preferred_element_type=jnp.float32)
    return context.astype(jnp.bfloat16)


def fill_pages(kv_rot, lengths_row, prompt_start, table_row, page_slots):
    page_count = table_row.shape[0]
    prompt_count = lengths_row.shape[0]
    per_prompt = page_count // prompt_count
    page_index = jnp.arange(page_count, dtype=jnp.int32)
    entry = jnp.sum(
        jnp.where(table_row[None, :] == page_index[:, None], page_index[None, :], 0), axis=1
    )
    prompt_of = entry // per_prompt
    page_of = entry % per_prompt
    prompt_numbers = jnp.arange(prompt_count, dtype=jnp.int32)
    chosen = prompt_of[:, None] == prompt_numbers[None, :]
    prompt_len = jnp.sum(jnp.where(chosen, lengths_row[None, :], 0), axis=1)
    base_row = jnp.sum(jnp.where(chosen, prompt_start[None, :], 0), axis=1)
    within = page_of[:, None] * page_slots + jnp.arange(page_slots, dtype=jnp.int32)[None, :]
    valid = within < prompt_len[:, None]
    source = jnp.minimum(base_row[:, None] + within, kv_rot.shape[0] - 1)
    return jnp.where(valid[:, :, None], kv_rot[source], jnp.zeros((), kv_rot.dtype))


def swap(x, axis_name):
    return lax.ppermute(x, axis_name, [(0, 1), (1, 0)])


def in_order(own, other, first):
    lower = jnp.where(first, own, other)
    upper = jnp.where(first, other, own)
    return lower, upper


def mp_gather(x, axis, mp_count):
    if mp_count == 2:
        lower, upper = in_order(x, swap(x, "mp"), lax.axis_index("mp") == 0)
        return jnp.concatenate([lower, upper], axis=axis)
    return lax.all_gather(x, "mp", axis=axis, tiled=True)


def half_of(x, axis, which):
    width = x.shape[axis] // 2
    return lax.dynamic_slice_in_dim(x, which * width, width, axis)


def shards(
    tokens,
    layer_norm_gain,
    layer_norm_bias,
    query_weight,
    key_value_weight,
    output_weight,
    adapter_down_factors,
    adapter_up_factors,
    lengths,
    prompt_adapter,
    prompt_page_table,
    adapter_storage,
    mp_count,
):
    side = lax.axis_index("dl")
    first = side == 0
    mp_index = lax.axis_index("mp")
    own_rows = tokens.shape[0]
    group_count = lengths.shape[0]
    group_rows = own_rows // group_count
    prompt_count = lengths.shape[1]
    pair_rows = 2 * own_rows

    normed = layer_norm(tokens, layer_norm_gain, layer_norm_bias)

    shard_rows = query_weight.shape[0]
    rank_width = adapter_down_factors.shape[2]
    kept = (
        half_of(query_weight, 1, side),
        key_value_weight,
        adapter_down_factors,
        half_of(adapter_up_factors, 2, side),
    )
    sent = (
        half_of(query_weight, 1, 1 - side),
        key_value_weight,
        adapter_down_factors,
        half_of(adapter_up_factors, 2, 1 - side),
    )
    kept_cols = [pack_columns(part, shard_rows) for part in kept]
    widths = [part.shape[1] for part in kept_cols]
    kept_block = jnp.concatenate(kept_cols, axis=1)
    sent_block = jnp.concatenate([pack_columns(part, shard_rows) for part in sent], axis=1)
    lower, upper = in_order(kept_block, swap(sent_block, "dl"), first)
    gathered = lax.all_gather(jnp.stack([lower, upper]), "dh", axis=0, tiled=False)
    gathered = gathered.reshape((-1,) + gathered.shape[2:])
    offsets = [sum(widths[:i]) for i in range(len(widths))]
    unpacked = [
        unpack_columns(gathered[:, :, off : off + width], part.shape)
        for off, width, part in zip(offsets, widths, kept)
    ]
    query_cols, kv_weight, down_all, up_cols = unpacked

    out_kept = half_of(output_weight, 1, side)
    out_sent = half_of(output_weight, 1, 1 - side)
    lower, upper = in_order(out_kept, swap(out_sent, "dl"), first)
    out_gathered = lax.all_gather(jnp.stack([lower, upper]), "dh", axis=0, tiled=False)
    out_cols = row_major(out_gathered.reshape(-1, out_kept.shape[1]))

    row_half = own_rows // mp_count
    partner_piece = swap(lax.dynamic_slice_in_dim(normed, mp_index * row_half, row_half, 0), "dl")
    partner_normed = mp_gather(partner_piece, 0, mp_count)
    lower, upper = in_order(normed, partner_normed, first)
    normed_pair = jnp.concatenate([lower, upper], axis=0)
    small = jnp.concatenate([lengths, prompt_adapter], axis=1)
    lower, upper = in_order(small, swap(small, "dl"), first)
    small_pair = jnp.concatenate([lower, upper], axis=0)
    lengths_pair = small_pair[:, :prompt_count]
    adapter_pair = small_pair[:, prompt_count:]

    member_grouped, position_grouped, start_grouped, index_grouped = jax.vmap(
        lambda one_row: layout(one_row, group_rows)
    )(lengths_pair)
    pair_groups = 2 * group_count
    pair_prompts = pair_groups * prompt_count
    position = position_grouped.reshape(pair_rows)
    prompt_global = (
        index_grouped + (jnp.arange(pair_groups, dtype=jnp.int32) * prompt_count)[:, None]
    ).reshape(pair_rows)
    member = prompt_global[:, None] == jnp.arange(pair_prompts, dtype=jnp.int32)[None, :]

    adapter_count = adapter_storage.shape[0]
    adapter_numbers = jnp.arange(adapter_count, dtype=jnp.int32)
    adapters_flat = adapter_pair.reshape(pair_prompts)
    storage_slots = jnp.sum(
        jnp.where(adapter_numbers[None, :] == adapters_flat[:, None], adapter_storage[None, :], 0),
        axis=1,
    )
    slot_rows = down_all.shape[0]
    matches = (storage_slots[:, None] == jnp.arange(slot_rows, dtype=jnp.int32)[None, :]).astype(
        jnp.bfloat16
    )
    down_selected = jnp.einsum(
        "pn,ndr->pdr", matches, down_all, preferred_element_type=jnp.float32
    ).astype(jnp.bfloat16)
    up_selected = jnp.einsum(
        "pn,nrc->prc", matches, up_cols, preferred_element_type=jnp.float32
    ).astype(jnp.bfloat16)

    feature_columns = adapter_down_factors.shape[1]
    features = lax.dynamic_slice_in_dim(normed, mp_index * feature_columns, feature_columns, 1)
    own_prompts = group_count * prompt_count
    own_down = lax.dynamic_slice_in_dim(down_selected, (1 - first.astype(jnp.int32)) * own_prompts, own_prompts, 0)
    own_member = lax.dynamic_slice_in_dim(member, (1 - first.astype(jnp.int32)) * own_rows, own_rows, 0)
    own_member = lax.dynamic_slice_in_dim(own_member, (1 - first.astype(jnp.int32)) * own_prompts, own_prompts, 1)
    all_ranks = jnp.dot(
        features,
        jnp.transpose(own_down, (1, 0, 2)).reshape(feature_columns, own_prompts * rank_width),
        preferred_element_type=jnp.float32,
    ).reshape(own_rows, own_prompts, rank_width)
    rank_portion = jnp.sum(jnp.where(own_member[:, :, None], all_ranks, 0.0), axis=1)
    ranks = lax.psum(rank_portion, "mp").astype(jnp.bfloat16)
    lower, upper = in_order(ranks, swap(ranks, "dl"), first)
    ranks_pair = jnp.concatenate([lower, upper], axis=0)
    spread = jnp.where(member[:, :, None], ranks_pair[:, None, :], jnp.zeros((), jnp.bfloat16))
    adapted_queries = jnp.dot(
        spread.reshape(pair_rows, pair_prompts * rank_width),
        up_selected.reshape(pair_prompts * rank_width, -1),
        preferred_element_type=jnp.float32,
    )

    query_base = jnp.dot(normed_pair, query_cols, preferred_element_type=jnp.float32)
    kv_base = jnp.dot(normed_pair, kv_weight, preferred_element_type=jnp.float32)
    queries = rotate(
        (query_base + adapted_queries).reshape(pair_rows, -1, HEAD_SIZE), position
    ).astype(jnp.bfloat16)
    keys_rot = rotate(kv_base[:, None, :HEAD_SIZE], position)[:, 0, :]
    kv_rot = jnp.concatenate([keys_rot, kv_base[:, HEAD_SIZE:]], axis=1).astype(jnp.bfloat16)
    local_heads = queries.shape[1]
    queries_grouped = queries.reshape(pair_groups, group_rows, local_heads, HEAD_SIZE)
    kv_grouped = kv_rot.reshape(pair_groups, group_rows, 2 * HEAD_SIZE)
    context_grouped = jax.vmap(
        lambda q_part, kv_part, idx_part: attend(
            q_part, kv_part[:, :HEAD_SIZE], kv_part[:, HEAD_SIZE:], idx_part
        )
    )(queries_grouped, kv_grouped, index_grouped)
    context = context_grouped.reshape(pair_rows, local_heads * HEAD_SIZE)

    lower, upper = in_order(context, swap(context, "dl"), first)
    context_all = mp_gather(jnp.concatenate([lower, upper], axis=1), 1, mp_count)
    own_start = (1 - first.astype(jnp.int32)) * own_rows
    partner_start = first.astype(jnp.int32) * own_rows
    partner_out = jnp.dot(
        lax.dynamic_slice_in_dim(context_all, partner_start, own_rows, 0),
        out_cols,
        preferred_element_type=jnp.float32,
    ).astype(jnp.bfloat16)
    received_out = swap(partner_out, "dl")
    own_out = jnp.dot(
        lax.dynamic_slice_in_dim(context_all, own_start, own_rows, 0),
        out_cols,
        preferred_element_type=jnp.float32,
    ).astype(jnp.bfloat16)
    lower, upper = in_order(own_out, received_out, first)
    attn_proj = jnp.concatenate([lower, upper], axis=1)

    own_groups = lax.dynamic_slice_in_dim(kv_grouped, (1 - first.astype(jnp.int32)) * group_count, group_count, 0)
    own_starts = lax.dynamic_slice_in_dim(start_grouped, (1 - first.astype(jnp.int32)) * group_count, group_count, 0)
    cache_grouped = jax.vmap(
        lambda kv_part, len_part, start_part, table_part: fill_pages(
            kv_part, len_part, start_part, table_part, PAGE
        )
    )(own_groups, lengths, own_starts, prompt_page_table)
    kv_cache = cache_grouped.reshape(group_count * prompt_page_table.shape[1], PAGE, 2 * HEAD_SIZE)
    return (attn_proj, kv_cache)


def solution(mesh):
    dp_count = mesh.shape["dp"]
    mp_count = mesh.shape["mp"]
    pair_mesh = Mesh(
        mesh.devices.reshape(dp_count // 2, 2, mp_count), ("dh", "dl", "mp")
    )
    dp = ("dh", "dl")
    return jax.shard_map(
        functools.partial(shards, mp_count=mp_count),
        mesh=pair_mesh,
        in_specs=(
            P(dp, None),
            P(),
            P(),
            P(dp, "mp"),
            P(dp, None),
            P(dp, "mp"),
            P(dp, "mp", None),
            P(dp, None, "mp"),
            P(dp, None),
            P(dp, None),
            P(dp, None),
            P(),
        ),
        out_specs=(P(dp, "mp"), P(dp, None, None)),
        check_vma=False,
    )
```

```python
import functools
import math

import jax
import jax.numpy as jnp
from jax import lax
from jax.sharding import Mesh, PartitionSpec as P
from jax.experimental.layout import Layout, with_layout_constraint

HEAD_SIZE = 64
PAGE = 128


def pack_columns(part, shard_rows, padded_rows):
    flat = part.reshape(-1)
    width = -(-flat.shape[0] // shard_rows)
    flat = jnp.pad(flat, (0, width * shard_rows - flat.shape[0]))
    return jnp.pad(flat.reshape(shard_rows, width), ((0, padded_rows - shard_rows), (0, 0)))


def unpack_columns(block, shape, shard_rows):
    shard_count = block.shape[0]
    size = math.prod(shape)
    flat = block[:, :shard_rows, :].reshape(shard_count, -1)[:, :size]
    return flat.reshape((shard_count * shape[0],) + tuple(shape[1:]))


def pad_features(x, shard_count, padded_rows):
    rows, width = x.shape
    split = x.reshape(rows, shard_count, width // shard_count)
    split = jnp.pad(split, ((0, 0), (0, 0), (0, padded_rows - width // shard_count)))
    return split.reshape(rows, shard_count * padded_rows)


def row_major(x):
    return with_layout_constraint(x, Layout(major_to_minor=tuple(range(x.ndim))))


def layer_norm(tokens, layer_norm_gain, layer_norm_bias):
    values = tokens.astype(jnp.float32)
    row_mean = jnp.mean(values, axis=-1, keepdims=True)
    centred = values - row_mean
    row_var = jnp.mean(centred * centred, axis=-1, keepdims=True)
    scaled = centred * lax.rsqrt(row_var + 1e-05)
    return (
        scaled * layer_norm_gain.astype(jnp.float32) + layer_norm_bias.astype(jnp.float32)
    ).astype(jnp.bfloat16)


def layout(lengths_row, row_number_count):
    prompt_end = jnp.cumsum(lengths_row)
    prompt_start = prompt_end - lengths_row
    row_index = jnp.arange(row_number_count, dtype=jnp.int32)
    member = (row_index[:, None] >= prompt_start[None, :]) & (
        row_index[:, None] < prompt_end[None, :]
    )
    first_row = jnp.sum(jnp.where(member, prompt_start[None, :], 0), axis=1)
    prompt_numbers = jnp.arange(lengths_row.shape[0], dtype=jnp.int32)
    prompt_index = jnp.sum(jnp.where(member, prompt_numbers[None, :], 0), axis=1)
    position = (row_index - first_row).astype(jnp.float32)
    return (member, position, prompt_start, prompt_index)


def rotate(values, position):
    half_width = values.shape[-1] // 2
    frequency = jnp.exp(
        jnp.arange(half_width, dtype=jnp.float32) * (-math.log(10000.0) / half_width)
    )
    angles = position[:, None, None] * frequency[None, None, :]
    cosine = jnp.cos(angles)
    sine = jnp.sin(angles)
    leading = values[..., :half_width]
    trailing = values[..., half_width:]
    return jnp.concatenate(
        [leading * cosine - trailing * sine, trailing * cosine + leading * sine], axis=-1
    )


def attend(queries, keys_rot, values, prompt_index):
    row_number_count = queries.shape[0]
    head_width = queries.shape[2]
    row_index = jnp.arange(row_number_count, dtype=jnp.int32)
    allowed = (prompt_index[:, None] == prompt_index[None, :]) & (
        row_index[None, :] <= row_index[:, None]
    )
    scores = jnp.einsum("thd,sd->hts", queries, keys_rot, preferred_element_type=jnp.float32) * (
        1.0 / math.sqrt(head_width)
    )
    scores = jnp.where(allowed[None, :, :], scores, -jnp.inf)
    row_peak = jnp.max(scores, axis=-1, keepdims=True)
    weights = jnp.exp(scores - row_peak)
    probs = (weights / jnp.sum(weights, axis=-1, keepdims=True)).astype(jnp.bfloat16)
    context = jnp.einsum("hts,sd->thd", probs, values, preferred_element_type=jnp.float32)
    return context.astype(jnp.bfloat16)


def fill_pages(kv_rot, lengths_row, prompt_start, table_row, page_slots):
    page_count = table_row.shape[0]
    prompt_count = lengths_row.shape[0]
    per_prompt = page_count // prompt_count
    page_index = jnp.arange(page_count, dtype=jnp.int32)
    entry = jnp.sum(
        jnp.where(table_row[None, :] == page_index[:, None], page_index[None, :], 0), axis=1
    )
    prompt_of = entry // per_prompt
    page_of = entry % per_prompt
    prompt_numbers = jnp.arange(prompt_count, dtype=jnp.int32)
    chosen = prompt_of[:, None] == prompt_numbers[None, :]
    prompt_len = jnp.sum(jnp.where(chosen, lengths_row[None, :], 0), axis=1)
    base_row = jnp.sum(jnp.where(chosen, prompt_start[None, :], 0), axis=1)
    within = page_of[:, None] * page_slots + jnp.arange(page_slots, dtype=jnp.int32)[None, :]
    valid = within < prompt_len[:, None]
    source = jnp.minimum(base_row[:, None] + within, kv_rot.shape[0] - 1)
    return jnp.where(valid[:, :, None], kv_rot[source], jnp.zeros((), kv_rot.dtype))


def swap(x, axis_name):
    return lax.ppermute(x, axis_name, [(0, 1), (1, 0)])


def pair_join(own, other, own_slot, axis):
    size = own.shape[axis]
    shape = list(own.shape)
    shape[axis] = 2 * size
    joined = jnp.zeros(shape, own.dtype)
    joined = lax.dynamic_update_slice_in_dim(joined, own, own_slot * size, axis)
    return lax.dynamic_update_slice_in_dim(joined, other, (1 - own_slot) * size, axis)


def mp_gather(x, axis, mp_count):
    if mp_count == 2:
        return pair_join(x, swap(x, "mp"), lax.axis_index("mp"), axis)
    return lax.all_gather(x, "mp", axis=axis, tiled=True)


def half_of(x, axis, which):
    width = x.shape[axis] // 2
    return lax.dynamic_slice_in_dim(x, which * width, width, axis)


def shards(
    tokens,
    layer_norm_gain,
    layer_norm_bias,
    query_weight,
    key_value_weight,
    output_weight,
    adapter_down_factors,
    adapter_up_factors,
    lengths,
    prompt_adapter,
    prompt_page_table,
    adapter_storage,
    mp_count,
):
    side = lax.axis_index("dl")
    first = side == 0
    mp_index = lax.axis_index("mp")
    own_rows = tokens.shape[0]
    group_count = lengths.shape[0]
    group_rows = own_rows // group_count
    prompt_count = lengths.shape[1]
    pair_rows = 2 * own_rows

    normed = layer_norm(tokens, layer_norm_gain, layer_norm_bias)

    shard_rows = query_weight.shape[0]
    rank_width = adapter_down_factors.shape[2]
    kept = (
        half_of(query_weight, 1, side),
        key_value_weight,
        adapter_down_factors,
        half_of(adapter_up_factors, 2, side),
    )
    sent = (
        half_of(query_weight, 1, 1 - side),
        key_value_weight,
        adapter_down_factors,
        half_of(adapter_up_factors, 2, 1 - side),
    )
    padded_rows = -(-shard_rows // 16) * 16
    kept_cols = [pack_columns(part, shard_rows, padded_rows) for part in kept]
    widths = [part.shape[1] for part in kept_cols]
    kept_block = jnp.concatenate(kept_cols, axis=1)
    sent_block = jnp.concatenate(
        [pack_columns(part, shard_rows, padded_rows) for part in sent], axis=1
    )
    pair_block = pair_join(kept_block[None], swap(sent_block, "dl")[None], side, 0)
    gathered = lax.all_gather(pair_block, "dh", axis=0, tiled=False)
    gathered = row_major(gathered).reshape((-1,) + gathered.shape[2:])
    shard_count = gathered.shape[0]
    offsets = [sum(widths[:i]) for i in range(len(widths))]
    unpacked = [
        unpack_columns(gathered[:, :, off : off + width], part.shape, shard_rows)
        for off, width, part in zip(offsets, widths, kept)
    ]
    _, _, down_all, up_cols = unpacked
    projection_block = gathered.reshape(-1, gathered.shape[2])

    out_kept = half_of(output_weight, 1, side)
    out_sent = half_of(output_weight, 1, 1 - side)
    out_pair = pair_join(out_kept[None], swap(out_sent, "dl")[None], side, 0)
    out_gathered = row_major(lax.all_gather(out_pair, "dh", axis=0, tiled=False))
    out_cols = out_gathered.reshape(-1, out_kept.shape[1])

    row_half = own_rows // mp_count
    partner_piece = swap(lax.dynamic_slice_in_dim(normed, mp_index * row_half, row_half, 0), "dl")
    partner_normed = mp_gather(partner_piece, 0, mp_count)
    normed_pair = pair_join(
        pad_features(normed, shard_count, padded_rows),
        pad_features(partner_normed, shard_count, padded_rows),
        side,
        0,
    )
    small = jnp.concatenate([lengths, prompt_adapter], axis=1)
    small_pair = pair_join(small, swap(small, "dl"), side, 0)
    lengths_pair = small_pair[:, :prompt_count]
    adapter_pair = small_pair[:, prompt_count:]

    member_grouped, position_grouped, start_grouped, index_grouped = jax.vmap(
        lambda one_row: layout(one_row, group_rows)
    )(lengths_pair)
    pair_groups = 2 * group_count
    pair_prompts = pair_groups * prompt_count
    position = position_grouped.reshape(pair_rows)
    prompt_global = (
        index_grouped + (jnp.arange(pair_groups, dtype=jnp.int32) * prompt_count)[:, None]
    ).reshape(pair_rows)
    member = prompt_global[:, None] == jnp.arange(pair_prompts, dtype=jnp.int32)[None, :]

    adapter_count = adapter_storage.shape[0]
    adapter_numbers = jnp.arange(adapter_count, dtype=jnp.int32)
    adapters_flat = adapter_pair.reshape(pair_prompts)
    storage_slots = jnp.sum(
        jnp.where(adapter_numbers[None, :] == adapters_flat[:, None], adapter_storage[None, :], 0),
        axis=1,
    )
    slot_rows = down_all.shape[0]
    matches = (storage_slots[:, None] == jnp.arange(slot_rows, dtype=jnp.int32)[None, :]).astype(
        jnp.bfloat16
    )
    down_selected = jnp.einsum(
        "pn,ndr->pdr", matches, down_all, preferred_element_type=jnp.float32
    ).astype(jnp.bfloat16)
    up_selected = jnp.einsum(
        "pn,nrc->prc", matches, up_cols, preferred_element_type=jnp.float32
    ).astype(jnp.bfloat16)

    feature_columns = adapter_down_factors.shape[1]
    features = lax.dynamic_slice_in_dim(normed, mp_index * feature_columns, feature_columns, 1)
    own_prompts = group_count * prompt_count
    own_down = lax.dynamic_slice_in_dim(down_selected, (1 - first.astype(jnp.int32)) * own_prompts, own_prompts, 0)
    own_member = lax.dynamic_slice_in_dim(member, (1 - first.astype(jnp.int32)) * own_rows, own_rows, 0)
    own_member = lax.dynamic_slice_in_dim(own_member, (1 - first.astype(jnp.int32)) * own_prompts, own_prompts, 1)
    all_ranks = jnp.dot(
        features,
        jnp.transpose(own_down, (1, 0, 2)).reshape(feature_columns, own_prompts * rank_width),
        preferred_element_type=jnp.float32,
    ).reshape(own_rows, own_prompts, rank_width)
    rank_portion = jnp.sum(jnp.where(own_member[:, :, None], all_ranks, 0.0), axis=1)
    ranks = lax.psum(rank_portion, "mp").astype(jnp.bfloat16)
    ranks_pair = pair_join(ranks, swap(ranks, "dl"), side, 0)
    spread = jnp.where(member[:, :, None], ranks_pair[:, None, :], jnp.zeros((), jnp.bfloat16))
    adapted_queries = jnp.dot(
        spread.reshape(pair_rows, pair_prompts * rank_width),
        up_selected.reshape(pair_prompts * rank_width, -1),
        preferred_element_type=jnp.float32,
    )

    projected = jnp.dot(normed_pair, projection_block, preferred_element_type=jnp.float32)
    query_base = projected[:, : widths[0]]
    kv_base = projected[:, widths[0] : widths[0] + widths[1]]
    queries = rotate(
        (query_base + adapted_queries).reshape(pair_rows, -1, HEAD_SIZE), position
    ).astype(jnp.bfloat16)
    keys_rot = rotate(kv_base[:, None, :HEAD_SIZE], position)[:, 0, :]
    kv_rot = jnp.concatenate([keys_rot, kv_base[:, HEAD_SIZE:]], axis=1).astype(jnp.bfloat16)
    local_heads = queries.shape[1]
    queries_grouped = queries.reshape(pair_groups, group_rows, local_heads, HEAD_SIZE)
    kv_grouped = kv_rot.reshape(pair_groups, group_rows, 2 * HEAD_SIZE)
    context_grouped = jax.vmap(
        lambda q_part, kv_part, idx_part: attend(
            q_part, kv_part[:, :HEAD_SIZE], kv_part[:, HEAD_SIZE:], idx_part
        )
    )(queries_grouped, kv_grouped, index_grouped)
    context = context_grouped.reshape(pair_rows, local_heads * HEAD_SIZE)

    context_all = mp_gather(pair_join(context, swap(context, "dl"), side, 1), 1, mp_count)
    own_start = (1 - first.astype(jnp.int32)) * own_rows
    partner_start = first.astype(jnp.int32) * own_rows
    partner_out = jnp.dot(
        lax.dynamic_slice_in_dim(context_all, partner_start, own_rows, 0),
        out_cols,
        preferred_element_type=jnp.float32,
    ).astype(jnp.bfloat16)
    received_out = swap(partner_out, "dl")
    own_out = jnp.dot(
        lax.dynamic_slice_in_dim(context_all, own_start, own_rows, 0),
        out_cols,
        preferred_element_type=jnp.float32,
    ).astype(jnp.bfloat16)
    attn_proj = pair_join(own_out, received_out, side, 1)

    own_groups = lax.dynamic_slice_in_dim(kv_grouped, (1 - first.astype(jnp.int32)) * group_count, group_count, 0)
    own_starts = lax.dynamic_slice_in_dim(start_grouped, (1 - first.astype(jnp.int32)) * group_count, group_count, 0)
    cache_grouped = jax.vmap(
        lambda kv_part, len_part, start_part, table_part: fill_pages(
            kv_part, len_part, start_part, table_part, PAGE
        )
    )(own_groups, lengths, own_starts, prompt_page_table)
    kv_cache = cache_grouped.reshape(group_count * prompt_page_table.shape[1], PAGE, 2 * HEAD_SIZE)
    return (attn_proj, kv_cache)


def solution(mesh):
    dp_count = mesh.shape["dp"]
    mp_count = mesh.shape["mp"]
    pair_mesh = Mesh(
        mesh.devices.reshape(dp_count // 2, 2, mp_count), ("dh", "dl", "mp")
    )
    dp = ("dh", "dl")
    return jax.shard_map(
        functools.partial(shards, mp_count=mp_count),
        mesh=pair_mesh,
        in_specs=(
            P(dp, None),
            P(),
            P(),
            P(dp, "mp"),
            P(dp, None),
            P(dp, "mp"),
            P(dp, "mp", None),
            P(dp, None, "mp"),
            P(dp, None),
            P(dp, None),
            P(dp, None),
            P(),
        ),
        out_specs=(P(dp, "mp"), P(dp, None, None)),
        check_vma=False,
    )
```

```python
import functools
import math

import jax
import jax.numpy as jnp
from jax import lax
from jax.sharding import Mesh, PartitionSpec as P
from jax.experimental.layout import Layout, with_layout_constraint

HEAD_SIZE = 64
PAGE = 128


def pack_columns(part, shard_rows, padded_rows):
    flat = part.reshape(-1)
    width = -(-flat.shape[0] // shard_rows)
    flat = jnp.pad(flat, (0, width * shard_rows - flat.shape[0]))
    return jnp.pad(flat.reshape(shard_rows, width), ((0, padded_rows - shard_rows), (0, 0)))


def unpack_columns(block, shape, shard_rows):
    shard_count = block.shape[0]
    size = math.prod(shape)
    flat = block[:, :shard_rows, :].reshape(shard_count, -1)[:, :size]
    return flat.reshape((shard_count * shape[0],) + tuple(shape[1:]))


def pad_features(x, shard_count, padded_rows):
    rows, width = x.shape
    split = x.reshape(rows, shard_count, width // shard_count)
    split = jnp.pad(split, ((0, 0), (0, 0), (0, padded_rows - width // shard_count)))
    return split.reshape(rows, shard_count * padded_rows)


def row_major(x):
    return with_layout_constraint(x, Layout(major_to_minor=tuple(range(x.ndim))))


def layer_norm(tokens, layer_norm_gain, layer_norm_bias):
    values = tokens.astype(jnp.float32)
    row_mean = jnp.mean(values, axis=-1, keepdims=True)
    centred = values - row_mean
    row_var = jnp.mean(centred * centred, axis=-1, keepdims=True)
    scaled = centred * lax.rsqrt(row_var + 1e-05)
    return (
        scaled * layer_norm_gain.astype(jnp.float32) + layer_norm_bias.astype(jnp.float32)
    ).astype(jnp.bfloat16)


def layout(lengths_row, row_number_count):
    prompt_end = jnp.cumsum(lengths_row)
    prompt_start = prompt_end - lengths_row
    row_index = jnp.arange(row_number_count, dtype=jnp.int32)
    member = (row_index[:, None] >= prompt_start[None, :]) & (
        row_index[:, None] < prompt_end[None, :]
    )
    first_row = jnp.sum(jnp.where(member, prompt_start[None, :], 0), axis=1)
    prompt_numbers = jnp.arange(lengths_row.shape[0], dtype=jnp.int32)
    prompt_index = jnp.sum(jnp.where(member, prompt_numbers[None, :], 0), axis=1)
    position = (row_index - first_row).astype(jnp.float32)
    return (member, position, prompt_start, prompt_index)


def rotate(values, position):
    half_width = values.shape[-1] // 2
    frequency = jnp.exp(
        jnp.arange(half_width, dtype=jnp.float32) * (-math.log(10000.0) / half_width)
    )
    angles = position[:, None, None] * frequency[None, None, :]
    cosine = jnp.cos(angles)
    sine = jnp.sin(angles)
    leading = values[..., :half_width]
    trailing = values[..., half_width:]
    return jnp.concatenate(
        [leading * cosine - trailing * sine, trailing * cosine + leading * sine], axis=-1
    )


def attend(queries, keys_rot, values, prompt_index):
    row_number_count = queries.shape[0]
    head_width = queries.shape[2]
    row_index = jnp.arange(row_number_count, dtype=jnp.int32)
    allowed = (prompt_index[:, None] == prompt_index[None, :]) & (
        row_index[None, :] <= row_index[:, None]
    )
    scores = jnp.einsum("thd,sd->hts", queries, keys_rot, preferred_element_type=jnp.float32) * (
        1.0 / math.sqrt(head_width)
    )
    scores = jnp.where(allowed[None, :, :], scores, -jnp.inf)
    row_peak = jnp.max(scores, axis=-1, keepdims=True)
    weights = jnp.exp(scores - row_peak)
    probs = (weights / jnp.sum(weights, axis=-1, keepdims=True)).astype(jnp.bfloat16)
    context = jnp.einsum("hts,sd->thd", probs, values, preferred_element_type=jnp.float32)
    return context.astype(jnp.bfloat16)


def fill_pages(kv_rot, lengths_row, prompt_start, table_row, page_slots):
    page_count = table_row.shape[0]
    prompt_count = lengths_row.shape[0]
    per_prompt = page_count // prompt_count
    page_index = jnp.arange(page_count, dtype=jnp.int32)
    entry = jnp.sum(
        jnp.where(table_row[None, :] == page_index[:, None], page_index[None, :], 0), axis=1
    )
    prompt_of = entry // per_prompt
    page_of = entry % per_prompt
    prompt_numbers = jnp.arange(prompt_count, dtype=jnp.int32)
    chosen = prompt_of[:, None] == prompt_numbers[None, :]
    prompt_len = jnp.sum(jnp.where(chosen, lengths_row[None, :], 0), axis=1)
    base_row = jnp.sum(jnp.where(chosen, prompt_start[None, :], 0), axis=1)
    within = page_of[:, None] * page_slots + jnp.arange(page_slots, dtype=jnp.int32)[None, :]
    valid = within < prompt_len[:, None]
    source = jnp.minimum(base_row[:, None] + within, kv_rot.shape[0] - 1)
    return jnp.where(valid[:, :, None], kv_rot[source], jnp.zeros((), kv_rot.dtype))


def swap(x, axis_name):
    return lax.ppermute(x, axis_name, [(0, 1), (1, 0)])


def pair_join(own, other, own_slot, axis):
    first = own_slot == 0
    lower = jnp.where(first, own, other)
    upper = jnp.where(first, other, own)
    return jnp.concatenate([lower, upper], axis=axis)


def mp_gather(x, axis, mp_count):
    if mp_count == 2:
        return pair_join(x, swap(x, "mp"), lax.axis_index("mp"), axis)
    return lax.all_gather(x, "mp", axis=axis, tiled=True)


def mp_pieces(x, mp_count):
    if mp_count == 2:
        other = swap(x, "mp")
        first = lax.axis_index("mp") == 0
        return [jnp.where(first, x, other), jnp.where(first, other, x)]
    stacked = lax.all_gather(x, "mp", axis=0, tiled=False)
    return [stacked[m] for m in range(mp_count)]


def half_of(x, axis, which):
    width = x.shape[axis] // 2
    return lax.dynamic_slice_in_dim(x, which * width, width, axis)


def shards(
    tokens,
    layer_norm_gain,
    layer_norm_bias,
    query_weight,
    key_value_weight,
    output_weight,
    adapter_down_factors,
    adapter_up_factors,
    lengths,
    prompt_adapter,
    prompt_page_table,
    adapter_storage,
    mp_count,
):
    side = lax.axis_index("dl")
    mp_index = lax.axis_index("mp")
    own_rows = tokens.shape[0]
    group_count = lengths.shape[0]
    group_rows = own_rows // group_count
    prompt_count = lengths.shape[1]
    pair_rows = 2 * own_rows

    normed = layer_norm(tokens, layer_norm_gain, layer_norm_bias)

    shard_rows = query_weight.shape[0]
    rank_width = adapter_down_factors.shape[2]
    kept = (
        half_of(query_weight, 1, side),
        key_value_weight,
        adapter_down_factors,
        half_of(adapter_up_factors, 2, side),
    )
    sent = (
        half_of(query_weight, 1, 1 - side),
        key_value_weight,
        adapter_down_factors,
        half_of(adapter_up_factors, 2, 1 - side),
    )
    padded_rows = -(-shard_rows // 16) * 16
    kept_cols = [pack_columns(part, shard_rows, padded_rows) for part in kept]
    widths = [part.shape[1] for part in kept_cols]
    kept_block = jnp.concatenate(kept_cols, axis=1)
    sent_block = jnp.concatenate(
        [pack_columns(part, shard_rows, padded_rows) for part in sent], axis=1
    )
    pair_block = pair_join(kept_block[None], swap(sent_block, "dl")[None], side, 0)
    gathered = lax.all_gather(pair_block, "dh", axis=0, tiled=False)
    gathered = row_major(gathered).reshape((-1,) + gathered.shape[2:])
    shard_count = gathered.shape[0]
    offsets = [sum(widths[:i]) for i in range(len(widths))]
    unpacked = [
        unpack_columns(gathered[:, :, off : off + width], part.shape, shard_rows)
        for off, width, part in zip(offsets, widths, kept)
    ]
    _, _, down_all, up_cols = unpacked
    projection_block = gathered.reshape(-1, gathered.shape[2])

    out_kept = half_of(output_weight, 1, side)
    out_sent = half_of(output_weight, 1, 1 - side)
    out_pair = pair_join(out_kept[None], swap(out_sent, "dl")[None], side, 0)
    out_gathered = row_major(lax.all_gather(out_pair, "dh", axis=0, tiled=False))
    out_cols = out_gathered.reshape(-1, out_kept.shape[1])

    normed_padded = pad_features(normed, shard_count, padded_rows)
    row_half = own_rows // mp_count
    partner_piece = swap(
        lax.dynamic_slice_in_dim(normed_padded, mp_index * row_half, row_half, 0), "dl"
    )
    partner_normed = jnp.concatenate(mp_pieces(partner_piece, mp_count), axis=0)
    normed_pair = jnp.concatenate([normed_padded, partner_normed], axis=0)
    small = jnp.concatenate([lengths, prompt_adapter], axis=1)
    small_pair = jnp.concatenate([small, swap(small, "dl")], axis=0)
    lengths_pair = small_pair[:, :prompt_count]
    adapter_pair = small_pair[:, prompt_count:]

    member_grouped, position_grouped, start_grouped, index_grouped = jax.vmap(
        lambda one_row: layout(one_row, group_rows)
    )(lengths_pair)
    pair_groups = 2 * group_count
    pair_prompts = pair_groups * prompt_count
    own_prompts = group_count * prompt_count
    position = position_grouped.reshape(pair_rows)
    prompt_global = (
        index_grouped + (jnp.arange(pair_groups, dtype=jnp.int32) * prompt_count)[:, None]
    ).reshape(pair_rows)
    member = prompt_global[:, None] == jnp.arange(pair_prompts, dtype=jnp.int32)[None, :]

    adapter_count = adapter_storage.shape[0]
    adapter_numbers = jnp.arange(adapter_count, dtype=jnp.int32)
    adapters_flat = adapter_pair.reshape(pair_prompts)
    storage_slots = jnp.sum(
        jnp.where(adapter_numbers[None, :] == adapters_flat[:, None], adapter_storage[None, :], 0),
        axis=1,
    )
    slot_rows = down_all.shape[0]
    matches = (storage_slots[:, None] == jnp.arange(slot_rows, dtype=jnp.int32)[None, :]).astype(
        jnp.bfloat16
    )
    down_selected = jnp.einsum(
        "pn,ndr->pdr", matches[:own_prompts], down_all, preferred_element_type=jnp.float32
    ).astype(jnp.bfloat16)
    up_selected = jnp.einsum(
        "pn,nrc->prc", matches, up_cols, preferred_element_type=jnp.float32
    ).astype(jnp.bfloat16)

    feature_columns = adapter_down_factors.shape[1]
    features = lax.dynamic_slice_in_dim(normed, mp_index * feature_columns, feature_columns, 1)
    own_member = member[:own_rows, :own_prompts]
    all_ranks = jnp.dot(
        features,
        jnp.transpose(down_selected, (1, 0, 2)).reshape(feature_columns, own_prompts * rank_width),
        preferred_element_type=jnp.float32,
    ).reshape(own_rows, own_prompts, rank_width)
    rank_portion = jnp.sum(jnp.where(own_member[:, :, None], all_ranks, 0.0), axis=1)
    ranks = lax.psum(rank_portion, "mp").astype(jnp.bfloat16)
    ranks_pair = jnp.concatenate([ranks, swap(ranks, "dl")], axis=0)
    spread = jnp.where(member[:, :, None], ranks_pair[:, None, :], jnp.zeros((), jnp.bfloat16))
    adapted_queries = jnp.dot(
        spread.reshape(pair_rows, pair_prompts * rank_width),
        up_selected.reshape(pair_prompts * rank_width, -1),
        preferred_element_type=jnp.float32,
    )

    projected = jnp.dot(normed_pair, projection_block, preferred_element_type=jnp.float32)
    query_base = projected[:, : widths[0]]
    kv_base = projected[:, widths[0] : widths[0] + widths[1]]
    queries = rotate(
        (query_base + adapted_queries).reshape(pair_rows, -1, HEAD_SIZE), position
    ).astype(jnp.bfloat16)
    keys_rot = rotate(kv_base[:, None, :HEAD_SIZE], position)[:, 0, :]
    kv_rot = jnp.concatenate([keys_rot, kv_base[:, HEAD_SIZE:]], axis=1).astype(jnp.bfloat16)
    local_heads = queries.shape[1]
    queries_grouped = queries.reshape(pair_groups, group_rows, local_heads, HEAD_SIZE)
    kv_grouped = kv_rot.reshape(pair_groups, group_rows, 2 * HEAD_SIZE)
    context_grouped = jax.vmap(
        lambda q_part, kv_part, idx_part: attend(
            q_part, kv_part[:, :HEAD_SIZE], kv_part[:, HEAD_SIZE:], idx_part
        )
    )(queries_grouped, kv_grouped, index_grouped)
    context = context_grouped.reshape(pair_rows, local_heads * HEAD_SIZE)

    partner_context = swap(context, "dl")
    partner_context = jnp.concatenate(
        [partner_context[own_rows:], partner_context[:own_rows]], axis=0
    )
    chip_context = jnp.stack([context, partner_context])
    pieces = mp_pieces(chip_context, mp_count)
    block = context.shape[1]

    def project(row_start):
        total = None
        for m in range(mp_count):
            for which in range(2):
                quarter = 2 * m + jnp.where(which == 0, side, 1 - side)
                rows = lax.dynamic_slice_in_dim(out_cols, quarter * block, block, 0)
                part = jnp.dot(
                    pieces[m][which, row_start : row_start + own_rows],
                    rows,
                    preferred_element_type=jnp.float32,
                )
                total = part if total is None else total + part
        return total.astype(jnp.bfloat16)

    received_out = swap(project(own_rows), "dl")
    own_out = project(0)
    attn_proj = pair_join(own_out, received_out, side, 1)

    cache_grouped = jax.vmap(
        lambda kv_part, len_part, start_part, table_part: fill_pages(
            kv_part, len_part, start_part, table_part, PAGE
        )
    )(kv_grouped[:group_count], lengths, start_grouped[:group_count], prompt_page_table)
    kv_cache = cache_grouped.reshape(group_count * prompt_page_table.shape[1], PAGE, 2 * HEAD_SIZE)
    return (attn_proj, kv_cache)


def solution(mesh):
    dp_count = mesh.shape["dp"]
    mp_count = mesh.shape["mp"]
    pair_mesh = Mesh(
        mesh.devices.reshape(dp_count // 2, 2, mp_count), ("dh", "dl", "mp")
    )
    dp = ("dh", "dl")
    return jax.shard_map(
        functools.partial(shards, mp_count=mp_count),
        mesh=pair_mesh,
        in_specs=(
            P(dp, None),
            P(),
            P(),
            P(dp, "mp"),
            P(dp, None),
            P(dp, "mp"),
            P(dp, "mp", None),
            P(dp, None, "mp"),
            P(dp, None),
            P(dp, None),
            P(dp, None),
            P(),
        ),
        out_specs=(P(dp, "mp"), P(dp, None, None)),
        check_vma=False,
    )
```

```python
import functools
import math

import jax
import jax.numpy as jnp
from jax import lax
from jax.sharding import Mesh, PartitionSpec as P
from jax.experimental.layout import Layout, with_layout_constraint

HEAD_SIZE = 64
PAGE = 128


def pack_columns(part, shard_rows, padded_rows):
    flat = part.reshape(-1)
    width = -(-flat.shape[0] // shard_rows)
    flat = jnp.pad(flat, (0, width * shard_rows - flat.shape[0]))
    return jnp.pad(flat.reshape(shard_rows, width), ((0, padded_rows - shard_rows), (0, 0)))


def unpack_columns(block, shape, shard_rows):
    shard_count = block.shape[0]
    size = math.prod(shape)
    flat = block[:, :shard_rows, :].reshape(shard_count, -1)[:, :size]
    return flat.reshape((shard_count * shape[0],) + tuple(shape[1:]))


def pad_features(x, shard_count, padded_rows):
    rows, width = x.shape
    split = x.reshape(rows, shard_count, width // shard_count)
    split = jnp.pad(split, ((0, 0), (0, 0), (0, padded_rows - width // shard_count)))
    return split.reshape(rows, shard_count * padded_rows)


def row_major(x):
    return with_layout_constraint(x, Layout(major_to_minor=tuple(range(x.ndim))))


def layer_norm(tokens, layer_norm_gain, layer_norm_bias):
    values = tokens.astype(jnp.float32)
    row_mean = jnp.mean(values, axis=-1, keepdims=True)
    centred = values - row_mean
    row_var = jnp.mean(centred * centred, axis=-1, keepdims=True)
    scaled = centred * lax.rsqrt(row_var + 1e-05)
    return (
        scaled * layer_norm_gain.astype(jnp.float32) + layer_norm_bias.astype(jnp.float32)
    ).astype(jnp.bfloat16)


def layout(lengths_row, row_number_count):
    prompt_end = jnp.cumsum(lengths_row)
    prompt_start = prompt_end - lengths_row
    row_index = jnp.arange(row_number_count, dtype=jnp.int32)
    member = (row_index[:, None] >= prompt_start[None, :]) & (
        row_index[:, None] < prompt_end[None, :]
    )
    first_row = jnp.sum(jnp.where(member, prompt_start[None, :], 0), axis=1)
    prompt_numbers = jnp.arange(lengths_row.shape[0], dtype=jnp.int32)
    prompt_index = jnp.sum(jnp.where(member, prompt_numbers[None, :], 0), axis=1)
    position = (row_index - first_row).astype(jnp.float32)
    return (member, position, prompt_start, prompt_index)


def rotate(values, position):
    half_width = values.shape[-1] // 2
    frequency = jnp.exp(
        jnp.arange(half_width, dtype=jnp.float32) * (-math.log(10000.0) / half_width)
    )
    angles = position[:, None, None] * frequency[None, None, :]
    cosine = jnp.cos(angles)
    sine = jnp.sin(angles)
    leading = values[..., :half_width]
    trailing = values[..., half_width:]
    return jnp.concatenate(
        [leading * cosine - trailing * sine, trailing * cosine + leading * sine], axis=-1
    )


def attend(queries, keys_rot, values, prompt_index):
    row_number_count = queries.shape[0]
    head_width = queries.shape[2]
    row_index = jnp.arange(row_number_count, dtype=jnp.int32)
    allowed = (prompt_index[:, None] == prompt_index[None, :]) & (
        row_index[None, :] <= row_index[:, None]
    )
    scores = jnp.einsum("thd,sd->hts", queries, keys_rot, preferred_element_type=jnp.float32) * (
        1.0 / math.sqrt(head_width)
    )
    scores = jnp.where(allowed[None, :, :], scores, -jnp.inf)
    row_peak = jnp.max(scores, axis=-1, keepdims=True)
    weights = jnp.exp(scores - row_peak)
    probs = (weights / jnp.sum(weights, axis=-1, keepdims=True)).astype(jnp.bfloat16)
    context = jnp.einsum("hts,sd->thd", probs, values, preferred_element_type=jnp.float32)
    return context.astype(jnp.bfloat16)


def fill_pages(kv_rot, lengths_row, prompt_start, table_row, page_slots):
    page_count = table_row.shape[0]
    prompt_count = lengths_row.shape[0]
    per_prompt = page_count // prompt_count
    page_index = jnp.arange(page_count, dtype=jnp.int32)
    entry = jnp.sum(
        jnp.where(table_row[None, :] == page_index[:, None], page_index[None, :], 0), axis=1
    )
    prompt_of = entry // per_prompt
    page_of = entry % per_prompt
    prompt_numbers = jnp.arange(prompt_count, dtype=jnp.int32)
    chosen = prompt_of[:, None] == prompt_numbers[None, :]
    prompt_len = jnp.sum(jnp.where(chosen, lengths_row[None, :], 0), axis=1)
    base_row = jnp.sum(jnp.where(chosen, prompt_start[None, :], 0), axis=1)
    within = page_of[:, None] * page_slots + jnp.arange(page_slots, dtype=jnp.int32)[None, :]
    valid = within < prompt_len[:, None]
    source = jnp.minimum(base_row[:, None] + within, kv_rot.shape[0] - 1)
    return jnp.where(valid[:, :, None], kv_rot[source], jnp.zeros((), kv_rot.dtype))


def swap(x, axis_name):
    return lax.ppermute(x, axis_name, [(0, 1), (1, 0)])


def pair_join(own, other, own_slot, axis):
    first = own_slot == 0
    lower = jnp.where(first, own, other)
    upper = jnp.where(first, other, own)
    return jnp.concatenate([lower, upper], axis=axis)


def mp_gather(x, axis, mp_count):
    if mp_count == 2:
        return pair_join(x, swap(x, "mp"), lax.axis_index("mp"), axis)
    return lax.all_gather(x, "mp", axis=axis, tiled=True)


def mp_pieces(x, mp_count):
    if mp_count == 2:
        other = swap(x, "mp")
        first = lax.axis_index("mp") == 0
        return [jnp.where(first, x, other), jnp.where(first, other, x)]
    stacked = lax.all_gather(x, "mp", axis=0, tiled=False)
    return [stacked[m] for m in range(mp_count)]


def half_of(x, axis, which):
    width = x.shape[axis] // 2
    return lax.dynamic_slice_in_dim(x, which * width, width, axis)


def shards(
    tokens,
    layer_norm_gain,
    layer_norm_bias,
    query_weight,
    key_value_weight,
    output_weight,
    adapter_down_factors,
    adapter_up_factors,
    lengths,
    prompt_adapter,
    prompt_page_table,
    adapter_storage,
    mp_count,
):
    side = lax.axis_index("dl")
    mp_index = lax.axis_index("mp")
    own_rows = tokens.shape[0]
    group_count = lengths.shape[0]
    group_rows = own_rows // group_count
    prompt_count = lengths.shape[1]
    pair_rows = 2 * own_rows

    normed = layer_norm(tokens, layer_norm_gain, layer_norm_bias)

    shard_rows = query_weight.shape[0]
    rank_width = adapter_down_factors.shape[2]
    down_by_rank = jnp.swapaxes(adapter_down_factors, 1, 2)
    kept = (
        half_of(query_weight, 1, side),
        key_value_weight,
        down_by_rank,
        half_of(adapter_up_factors, 2, side),
    )
    sent = (
        half_of(query_weight, 1, 1 - side),
        key_value_weight,
        down_by_rank,
        half_of(adapter_up_factors, 2, 1 - side),
    )
    padded_rows = -(-shard_rows // 16) * 16
    kept_cols = [pack_columns(part, shard_rows, padded_rows) for part in kept]
    widths = [part.shape[1] for part in kept_cols]
    kept_block = jnp.concatenate(kept_cols, axis=1)
    sent_block = jnp.concatenate(
        [pack_columns(part, shard_rows, padded_rows) for part in sent], axis=1
    )
    pair_block = pair_join(kept_block[None], swap(sent_block, "dl")[None], side, 0)
    gathered = lax.all_gather(pair_block, "dh", axis=0, tiled=False)
    gathered = row_major(gathered).reshape((-1,) + gathered.shape[2:])
    shard_count = gathered.shape[0]
    offsets = [sum(widths[:i]) for i in range(len(widths))]
    unpacked = [
        unpack_columns(gathered[:, :, off : off + width], part.shape, shard_rows)
        for off, width, part in zip(offsets, widths, kept)
    ]
    _, _, down_all, up_cols = unpacked
    projection_block = gathered.reshape(-1, gathered.shape[2])

    out_kept = half_of(output_weight, 1, side)
    out_sent = half_of(output_weight, 1, 1 - side)
    out_pair = pair_join(out_kept[None], swap(out_sent, "dl")[None], side, 0)
    out_gathered = lax.all_gather(out_pair, "dh", axis=0, tiled=False)
    heads_per_block = out_gathered.shape[0] * out_gathered.shape[1] // (2 * mp_count)

    normed_padded = pad_features(normed, shard_count, padded_rows)
    row_half = own_rows // mp_count
    partner_piece = swap(
        lax.dynamic_slice_in_dim(normed_padded, mp_index * row_half, row_half, 0), "dl"
    )
    partner_normed = jnp.concatenate(mp_pieces(partner_piece, mp_count), axis=0)
    normed_pair = jnp.concatenate([normed_padded, partner_normed], axis=0)
    small = jnp.concatenate([lengths, prompt_adapter], axis=1)
    small_pair = jnp.concatenate([small, swap(small, "dl")], axis=0)
    lengths_pair = small_pair[:, :prompt_count]
    adapter_pair = small_pair[:, prompt_count:]

    member_grouped, position_grouped, start_grouped, index_grouped = jax.vmap(
        lambda one_row: layout(one_row, group_rows)
    )(lengths_pair)
    pair_groups = 2 * group_count
    pair_prompts = pair_groups * prompt_count
    own_prompts = group_count * prompt_count
    position = position_grouped.reshape(pair_rows)
    prompt_global = (
        index_grouped + (jnp.arange(pair_groups, dtype=jnp.int32) * prompt_count)[:, None]
    ).reshape(pair_rows)
    member = prompt_global[:, None] == jnp.arange(pair_prompts, dtype=jnp.int32)[None, :]

    adapter_count = adapter_storage.shape[0]
    adapter_numbers = jnp.arange(adapter_count, dtype=jnp.int32)
    adapters_flat = adapter_pair.reshape(pair_prompts)
    storage_slots = jnp.sum(
        jnp.where(adapter_numbers[None, :] == adapters_flat[:, None], adapter_storage[None, :], 0),
        axis=1,
    )
    slot_rows = down_all.shape[0]
    matches = (storage_slots[:, None] == jnp.arange(slot_rows, dtype=jnp.int32)[None, :]).astype(
        jnp.bfloat16
    )
    down_selected = jnp.einsum(
        "pn,nrd->prd", matches[:own_prompts], down_all, preferred_element_type=jnp.float32
    ).astype(jnp.bfloat16)
    up_selected = jnp.einsum(
        "pn,nrc->prc", matches, up_cols, preferred_element_type=jnp.float32
    ).astype(jnp.bfloat16)

    feature_columns = adapter_down_factors.shape[1]
    features = lax.dynamic_slice_in_dim(normed, mp_index * feature_columns, feature_columns, 1)
    own_member = member[:own_rows, :own_prompts]
    all_ranks = jnp.einsum(
        "tf,qf->tq",
        features,
        down_selected.reshape(own_prompts * rank_width, feature_columns),
        preferred_element_type=jnp.float32,
    ).reshape(own_rows, own_prompts, rank_width)
    rank_portion = jnp.sum(jnp.where(own_member[:, :, None], all_ranks, 0.0), axis=1)
    ranks = lax.psum(rank_portion, "mp").astype(jnp.bfloat16)
    ranks_pair = jnp.concatenate([ranks, swap(ranks, "dl")], axis=0)
    spread = jnp.where(member[:, :, None], ranks_pair[:, None, :], jnp.zeros((), jnp.bfloat16))
    adapted_queries = jnp.dot(
        spread.reshape(pair_rows, pair_prompts * rank_width),
        up_selected.reshape(pair_prompts * rank_width, -1),
        preferred_element_type=jnp.float32,
    )

    projected = jnp.dot(normed_pair, projection_block, preferred_element_type=jnp.float32)
    query_base = projected[:, : widths[0]]
    kv_base = projected[:, widths[0] : widths[0] + widths[1]]
    queries = rotate(
        (query_base + adapted_queries).reshape(pair_rows, -1, HEAD_SIZE), position
    ).astype(jnp.bfloat16)
    keys_rot = rotate(kv_base[:, None, :HEAD_SIZE], position)[:, 0, :]
    kv_rot = jnp.concatenate([keys_rot, kv_base[:, HEAD_SIZE:]], axis=1).astype(jnp.bfloat16)
    local_heads = queries.shape[1]
    queries_grouped = queries.reshape(pair_groups, group_rows, local_heads, HEAD_SIZE)
    kv_grouped = kv_rot.reshape(pair_groups, group_rows, 2 * HEAD_SIZE)
    context_grouped = jax.vmap(
        lambda q_part, kv_part, idx_part: attend(
            q_part, kv_part[:, :HEAD_SIZE], kv_part[:, HEAD_SIZE:], idx_part
        )
    )(queries_grouped, kv_grouped, index_grouped)
    context = context_grouped.reshape(pair_rows, local_heads * HEAD_SIZE)

    partner_context = swap(context, "dl")
    partner_context = jnp.concatenate(
        [partner_context[own_rows:], partner_context[:own_rows]], axis=0
    )
    block = context.shape[1]
    if mp_count == 2:
        other_mp = 1 - mp_index
        pieces = [
            (context, 2 * mp_index + side),
            (swap(context, "mp"), 2 * other_mp + side),
            (partner_context, 2 * mp_index + 1 - side),
            (swap(partner_context, "mp"), 2 * other_mp + 1 - side),
        ]
    else:
        stacked = lax.all_gather(jnp.stack([context, partner_context]), "mp", axis=0, tiled=False)
        pieces = [
            (stacked[m, which], 2 * m + jnp.where(which == 0, side, 1 - side))
            for which in range(2)
            for m in range(mp_count)
        ]

    def project(row_start):
        total = None
        for piece, quarter in pieces:
            rows = lax.dynamic_slice_in_dim(out_gathered, quarter * (heads_per_block // 2), heads_per_block // 2, 0)
            part = jnp.einsum(
                "tabk,abkn->tn",
                piece[row_start : row_start + own_rows].reshape((own_rows,) + rows.shape[:3]),
                rows,
                preferred_element_type=jnp.float32,
            )
            total = part if total is None else total + part
        return total.astype(jnp.bfloat16)

    received_out = swap(project(own_rows), "dl")
    own_out = project(0)
    attn_proj = pair_join(own_out, received_out, side, 1)

    cache_grouped = jax.vmap(
        lambda kv_part, len_part, start_part, table_part: fill_pages(
            kv_part, len_part, start_part, table_part, PAGE
        )
    )(kv_grouped[:group_count], lengths, start_grouped[:group_count], prompt_page_table)
    kv_cache = cache_grouped.reshape(group_count * prompt_page_table.shape[1], PAGE, 2 * HEAD_SIZE)
    return (attn_proj, kv_cache)


def solution(mesh):
    dp_count = mesh.shape["dp"]
    mp_count = mesh.shape["mp"]
    pair_mesh = Mesh(
        mesh.devices.reshape(dp_count // 2, 2, mp_count), ("dh", "dl", "mp")
    )
    dp = ("dh", "dl")
    return jax.shard_map(
        functools.partial(shards, mp_count=mp_count),
        mesh=pair_mesh,
        in_specs=(
            P(dp, None),
            P(),
            P(),
            P(dp, "mp"),
            P(dp, None),
            P(dp, "mp"),
            P(dp, "mp", None),
            P(dp, None, "mp"),
            P(dp, None),
            P(dp, None),
            P(dp, None),
            P(),
        ),
        out_specs=(P(dp, "mp"), P(dp, None, None)),
        check_vma=False,
    )
```

```python
import functools
import math

import jax
import jax.numpy as jnp
from jax import lax
from jax.sharding import Mesh, PartitionSpec as P
from jax.experimental.layout import Layout, with_layout_constraint

HEAD_SIZE = 64
PAGE = 128


def pack_columns(part, shard_rows, padded_rows):
    flat = part.reshape(-1)
    width = -(-flat.shape[0] // shard_rows)
    flat = jnp.pad(flat, (0, width * shard_rows - flat.shape[0]))
    return jnp.pad(flat.reshape(shard_rows, width), ((0, padded_rows - shard_rows), (0, 0)))


def unpack_columns(block, shape, shard_rows):
    shard_count = block.shape[0]
    size = math.prod(shape)
    flat = block[:, :shard_rows, :].reshape(shard_count, -1)[:, :size]
    return flat.reshape((shard_count * shape[0],) + tuple(shape[1:]))


def pad_features(x, shard_count, padded_rows):
    rows, width = x.shape
    split = x.reshape(rows, shard_count, width // shard_count)
    split = jnp.pad(split, ((0, 0), (0, 0), (0, padded_rows - width // shard_count)))
    return split.reshape(rows, shard_count * padded_rows)


def row_major(x):
    return with_layout_constraint(x, Layout(major_to_minor=tuple(range(x.ndim))))


def layer_norm(tokens, layer_norm_gain, layer_norm_bias):
    values = tokens.astype(jnp.float32)
    row_mean = jnp.mean(values, axis=-1, keepdims=True)
    centred = values - row_mean
    row_var = jnp.mean(centred * centred, axis=-1, keepdims=True)
    scaled = centred * lax.rsqrt(row_var + 1e-05)
    return (
        scaled * layer_norm_gain.astype(jnp.float32) + layer_norm_bias.astype(jnp.float32)
    ).astype(jnp.bfloat16)


def layout(lengths_row, row_number_count):
    prompt_end = jnp.cumsum(lengths_row)
    prompt_start = prompt_end - lengths_row
    row_index = jnp.arange(row_number_count, dtype=jnp.int32)
    member = (row_index[:, None] >= prompt_start[None, :]) & (
        row_index[:, None] < prompt_end[None, :]
    )
    first_row = jnp.sum(jnp.where(member, prompt_start[None, :], 0), axis=1)
    prompt_numbers = jnp.arange(lengths_row.shape[0], dtype=jnp.int32)
    prompt_index = jnp.sum(jnp.where(member, prompt_numbers[None, :], 0), axis=1)
    position = (row_index - first_row).astype(jnp.float32)
    return (member, position, prompt_start, prompt_index)


def rotate(values, position):
    half_width = values.shape[-1] // 2
    frequency = jnp.exp(
        jnp.arange(half_width, dtype=jnp.float32) * (-math.log(10000.0) / half_width)
    )
    angles = position[:, None, None] * frequency[None, None, :]
    cosine = jnp.cos(angles)
    sine = jnp.sin(angles)
    leading = values[..., :half_width]
    trailing = values[..., half_width:]
    return jnp.concatenate(
        [leading * cosine - trailing * sine, trailing * cosine + leading * sine], axis=-1
    )


def attend(queries, keys_rot, values, prompt_index):
    row_number_count = queries.shape[0]
    head_width = queries.shape[2]
    row_index = jnp.arange(row_number_count, dtype=jnp.int32)
    allowed = (prompt_index[:, None] == prompt_index[None, :]) & (
        row_index[None, :] <= row_index[:, None]
    )
    scores = jnp.einsum("thd,sd->hts", queries, keys_rot, preferred_element_type=jnp.float32) * (
        1.0 / math.sqrt(head_width)
    )
    scores = jnp.where(allowed[None, :, :], scores, -jnp.inf)
    row_peak = jnp.max(scores, axis=-1, keepdims=True)
    weights = jnp.exp(scores - row_peak)
    probs = (weights / jnp.sum(weights, axis=-1, keepdims=True)).astype(jnp.bfloat16)
    context = jnp.einsum("hts,sd->thd", probs, values, preferred_element_type=jnp.float32)
    return context.astype(jnp.bfloat16)


def fill_pages(kv_rot, lengths_row, prompt_start, table_row, page_slots):
    page_count = table_row.shape[0]
    prompt_count = lengths_row.shape[0]
    per_prompt = page_count // prompt_count
    page_index = jnp.arange(page_count, dtype=jnp.int32)
    entry = jnp.sum(
        jnp.where(table_row[None, :] == page_index[:, None], page_index[None, :], 0), axis=1
    )
    prompt_of = entry // per_prompt
    page_of = entry % per_prompt
    prompt_numbers = jnp.arange(prompt_count, dtype=jnp.int32)
    chosen = prompt_of[:, None] == prompt_numbers[None, :]
    prompt_len = jnp.sum(jnp.where(chosen, lengths_row[None, :], 0), axis=1)
    base_row = jnp.sum(jnp.where(chosen, prompt_start[None, :], 0), axis=1)
    within = page_of[:, None] * page_slots + jnp.arange(page_slots, dtype=jnp.int32)[None, :]
    valid = within < prompt_len[:, None]
    source = jnp.minimum(base_row[:, None] + within, kv_rot.shape[0] - 1)
    return jnp.where(valid[:, :, None], kv_rot[source], jnp.zeros((), kv_rot.dtype))


def swap(x, axis_name):
    return lax.ppermute(x, axis_name, [(0, 1), (1, 0)])


def pair_join(own, other, own_slot, axis):
    first = own_slot == 0
    lower = jnp.where(first, own, other)
    upper = jnp.where(first, other, own)
    return jnp.concatenate([lower, upper], axis=axis)


def mp_gather(x, axis, mp_count):
    if mp_count == 2:
        return pair_join(x, swap(x, "mp"), lax.axis_index("mp"), axis)
    return lax.all_gather(x, "mp", axis=axis, tiled=True)


def mp_pieces(x, mp_count):
    if mp_count == 2:
        other = swap(x, "mp")
        first = lax.axis_index("mp") == 0
        return [jnp.where(first, x, other), jnp.where(first, other, x)]
    stacked = lax.all_gather(x, "mp", axis=0, tiled=False)
    return [stacked[m] for m in range(mp_count)]


def half_of(x, axis, which):
    width = x.shape[axis] // 2
    return lax.dynamic_slice_in_dim(x, which * width, width, axis)


def shards(
    tokens,
    layer_norm_gain,
    layer_norm_bias,
    query_weight,
    key_value_weight,
    output_weight,
    adapter_down_factors,
    adapter_up_factors,
    lengths,
    prompt_adapter,
    prompt_page_table,
    adapter_storage,
    mp_count,
):
    side = lax.axis_index("dl")
    mp_index = lax.axis_index("mp")
    own_rows = tokens.shape[0]
    group_count = lengths.shape[0]
    group_rows = own_rows // group_count
    prompt_count = lengths.shape[1]
    pair_rows = 2 * own_rows

    normed = layer_norm(tokens, layer_norm_gain, layer_norm_bias)

    shard_rows = query_weight.shape[0]
    rank_width = adapter_down_factors.shape[2]
    down_by_rank = jnp.swapaxes(adapter_down_factors, 1, 2)
    kept = (
        half_of(query_weight, 1, side),
        key_value_weight,
        down_by_rank,
        half_of(adapter_up_factors, 2, side),
    )
    sent = (
        half_of(query_weight, 1, 1 - side),
        key_value_weight,
        down_by_rank,
        half_of(adapter_up_factors, 2, 1 - side),
    )
    padded_rows = -(-shard_rows // 16) * 16
    kept_cols = [pack_columns(part, shard_rows, padded_rows) for part in kept]
    widths = [part.shape[1] for part in kept_cols]
    kept_block = jnp.concatenate(kept_cols, axis=1)
    sent_block = jnp.concatenate(
        [pack_columns(part, shard_rows, padded_rows) for part in sent], axis=1
    )
    pair_block = pair_join(kept_block[None], swap(sent_block, "dl")[None], side, 0)
    gathered = lax.all_gather(pair_block, "dh", axis=0, tiled=False)
    gathered = row_major(gathered).reshape((-1,) + gathered.shape[2:])
    shard_count = gathered.shape[0]
    offsets = [sum(widths[:i]) for i in range(len(widths))]
    unpacked = [
        unpack_columns(gathered[:, :, off : off + width], part.shape, shard_rows)
        for off, width, part in zip(offsets, widths, kept)
    ]
    _, _, down_all, up_cols = unpacked
    projection_block = gathered.reshape(-1, gathered.shape[2])

    out_kept = half_of(output_weight, 1, side)
    out_sent = half_of(output_weight, 1, 1 - side)
    out_pair = pair_join(out_kept[None], swap(out_sent, "dl")[None], side, 0)
    out_gathered = lax.all_gather(out_pair, "dh", axis=0, tiled=False)

    normed_padded = pad_features(normed, shard_count, padded_rows)
    row_half = own_rows // mp_count
    partner_piece = swap(
        lax.dynamic_slice_in_dim(normed_padded, mp_index * row_half, row_half, 0), "dl"
    )
    partner_normed = jnp.concatenate(mp_pieces(partner_piece, mp_count), axis=0)
    normed_pair = jnp.concatenate([normed_padded, partner_normed], axis=0)
    small = jnp.concatenate([lengths, prompt_adapter], axis=1)
    small_pair = jnp.concatenate([small, swap(small, "dl")], axis=0)
    lengths_pair = small_pair[:, :prompt_count]
    adapter_pair = small_pair[:, prompt_count:]

    member_grouped, position_grouped, start_grouped, index_grouped = jax.vmap(
        lambda one_row: layout(one_row, group_rows)
    )(lengths_pair)
    pair_groups = 2 * group_count
    pair_prompts = pair_groups * prompt_count
    own_prompts = group_count * prompt_count
    position = position_grouped.reshape(pair_rows)
    prompt_global = (
        index_grouped + (jnp.arange(pair_groups, dtype=jnp.int32) * prompt_count)[:, None]
    ).reshape(pair_rows)
    member = prompt_global[:, None] == jnp.arange(pair_prompts, dtype=jnp.int32)[None, :]

    adapter_count = adapter_storage.shape[0]
    adapter_numbers = jnp.arange(adapter_count, dtype=jnp.int32)
    adapters_flat = adapter_pair.reshape(pair_prompts)
    storage_slots = jnp.sum(
        jnp.where(adapter_numbers[None, :] == adapters_flat[:, None], adapter_storage[None, :], 0),
        axis=1,
    )
    slot_rows = down_all.shape[0]
    matches = (storage_slots[:, None] == jnp.arange(slot_rows, dtype=jnp.int32)[None, :]).astype(
        jnp.bfloat16
    )
    down_selected = jnp.einsum(
        "pn,nrd->prd", matches[:own_prompts], down_all, preferred_element_type=jnp.float32
    ).astype(jnp.bfloat16)
    up_selected = jnp.einsum(
        "pn,nrc->prc", matches, up_cols, preferred_element_type=jnp.float32
    ).astype(jnp.bfloat16)

    feature_columns = adapter_down_factors.shape[1]
    features = lax.dynamic_slice_in_dim(normed, mp_index * feature_columns, feature_columns, 1)
    own_member = member[:own_rows, :own_prompts]
    all_ranks = jnp.einsum(
        "tf,qf->tq",
        features,
        down_selected.reshape(own_prompts * rank_width, feature_columns),
        preferred_element_type=jnp.float32,
    ).reshape(own_rows, own_prompts, rank_width)
    rank_portion = jnp.sum(jnp.where(own_member[:, :, None], all_ranks, 0.0), axis=1)
    ranks = lax.psum(rank_portion, "mp").astype(jnp.bfloat16)
    ranks_pair = jnp.concatenate([ranks, swap(ranks, "dl")], axis=0)
    spread = jnp.where(member[:, :, None], ranks_pair[:, None, :], jnp.zeros((), jnp.bfloat16))
    adapted_queries = jnp.dot(
        spread.reshape(pair_rows, pair_prompts * rank_width),
        up_selected.reshape(pair_prompts * rank_width, -1),
        preferred_element_type=jnp.float32,
    )

    projected = jnp.dot(normed_pair, projection_block, preferred_element_type=jnp.float32)
    query_base = projected[:, : widths[0]]
    kv_base = projected[:, widths[0] : widths[0] + widths[1]]
    queries = rotate(
        (query_base + adapted_queries).reshape(pair_rows, -1, HEAD_SIZE), position
    ).astype(jnp.bfloat16)
    keys_rot = rotate(kv_base[:, None, :HEAD_SIZE], position)[:, 0, :]
    kv_rot = jnp.concatenate([keys_rot, kv_base[:, HEAD_SIZE:]], axis=1).astype(jnp.bfloat16)
    local_heads = queries.shape[1]
    queries_grouped = queries.reshape(pair_groups, group_rows, local_heads, HEAD_SIZE)
    kv_grouped = kv_rot.reshape(pair_groups, group_rows, 2 * HEAD_SIZE)
    def attend_groups(group_slice):
        context_grouped = jax.vmap(
            lambda q_part, kv_part, idx_part: attend(
                q_part, kv_part[:, :HEAD_SIZE], kv_part[:, HEAD_SIZE:], idx_part
            )
        )(queries_grouped[group_slice], kv_grouped[group_slice], index_grouped[group_slice])
        return context_grouped.reshape(own_rows, local_heads * HEAD_SIZE)

    context_own = attend_groups(slice(0, group_count))
    from_partner_for_partner_rows = swap(context_own, "dl")
    context_partner_rows = attend_groups(slice(group_count, pair_groups))
    from_partner_for_own_rows = swap(context_partner_rows, "dl")
    block = context_own.shape[1]
    blocks_per_quarter = out_gathered.shape[0] * out_gathered.shape[1] // (2 * mp_count)

    def pieces_of(mine, theirs):
        if mp_count == 2:
            other_mp = 1 - mp_index
            return [
                (mine, 2 * mp_index + side),
                (swap(mine, "mp"), 2 * other_mp + side),
                (theirs, 2 * mp_index + 1 - side),
                (swap(theirs, "mp"), 2 * other_mp + 1 - side),
            ]
        stacked = lax.all_gather(jnp.stack([mine, theirs]), "mp", axis=0, tiled=False)
        return [
            (stacked[m, which], 2 * m + (side if which == 0 else 1 - side))
            for which in range(2)
            for m in range(mp_count)
        ]

    def project(pieces):
        total = None
        for piece, quarter in pieces:
            rows = lax.dynamic_slice_in_dim(
                out_gathered, quarter * (blocks_per_quarter // 2), blocks_per_quarter // 2, 0
            )
            part = jnp.einsum(
                "tabk,abkn->tn",
                piece.reshape((own_rows,) + rows.shape[:3]),
                rows,
                preferred_element_type=jnp.float32,
            )
            total = part if total is None else total + part
        return total.astype(jnp.bfloat16)

    received_out = swap(project(pieces_of(context_partner_rows, from_partner_for_partner_rows)), "dl")
    own_out = project(pieces_of(context_own, from_partner_for_own_rows))
    attn_proj = pair_join(own_out, received_out, side, 1)

    cache_grouped = jax.vmap(
        lambda kv_part, len_part, start_part, table_part: fill_pages(
            kv_part, len_part, start_part, table_part, PAGE
        )
    )(kv_grouped[:group_count], lengths, start_grouped[:group_count], prompt_page_table)
    kv_cache = cache_grouped.reshape(group_count * prompt_page_table.shape[1], PAGE, 2 * HEAD_SIZE)
    return (attn_proj, kv_cache)


def solution(mesh):
    dp_count = mesh.shape["dp"]
    mp_count = mesh.shape["mp"]
    pair_mesh = Mesh(
        mesh.devices.reshape(dp_count // 2, 2, mp_count), ("dh", "dl", "mp")
    )
    dp = ("dh", "dl")
    return jax.shard_map(
        functools.partial(shards, mp_count=mp_count),
        mesh=pair_mesh,
        in_specs=(
            P(dp, None),
            P(),
            P(),
            P(dp, "mp"),
            P(dp, None),
            P(dp, "mp"),
            P(dp, "mp", None),
            P(dp, None, "mp"),
            P(dp, None),
            P(dp, None),
            P(dp, None),
            P(),
        ),
        out_specs=(P(dp, "mp"), P(dp, None, None)),
        check_vma=False,
    )
```

```python
import functools
import math

import jax
import jax.numpy as jnp
from jax import lax
from jax.sharding import Mesh, PartitionSpec as P
from jax.experimental.layout import Layout, with_layout_constraint

HEAD_SIZE = 64
PAGE = 128


def pack_columns(part, shard_rows, padded_rows):
    flat = part.reshape(-1)
    width = -(-flat.shape[0] // shard_rows)
    flat = jnp.pad(flat, (0, width * shard_rows - flat.shape[0]))
    return jnp.pad(flat.reshape(shard_rows, width), ((0, padded_rows - shard_rows), (0, 0)))


def unpack_columns(block, shape, shard_rows):
    shard_count = block.shape[0]
    size = math.prod(shape)
    flat = block[:, :shard_rows, :].reshape(shard_count, -1)[:, :size]
    return flat.reshape((shard_count * shape[0],) + tuple(shape[1:]))


def pad_features(x, shard_count, padded_rows):
    rows, width = x.shape
    split = x.reshape(rows, shard_count, width // shard_count)
    split = jnp.pad(split, ((0, 0), (0, 0), (0, padded_rows - width // shard_count)))
    return split.reshape(rows, shard_count * padded_rows)


def row_major(x):
    return with_layout_constraint(x, Layout(major_to_minor=tuple(range(x.ndim))))


def layer_norm(tokens, layer_norm_gain, layer_norm_bias):
    values = tokens.astype(jnp.float32)
    row_mean = jnp.mean(values, axis=-1, keepdims=True)
    centred = values - row_mean
    row_var = jnp.mean(centred * centred, axis=-1, keepdims=True)
    scaled = centred * lax.rsqrt(row_var + 1e-05)
    return (
        scaled * layer_norm_gain.astype(jnp.float32) + layer_norm_bias.astype(jnp.float32)
    ).astype(jnp.bfloat16)


def layout(lengths_row, row_number_count):
    prompt_end = jnp.cumsum(lengths_row)
    prompt_start = prompt_end - lengths_row
    row_index = jnp.arange(row_number_count, dtype=jnp.int32)
    member = (row_index[:, None] >= prompt_start[None, :]) & (
        row_index[:, None] < prompt_end[None, :]
    )
    first_row = jnp.sum(jnp.where(member, prompt_start[None, :], 0), axis=1)
    prompt_numbers = jnp.arange(lengths_row.shape[0], dtype=jnp.int32)
    prompt_index = jnp.sum(jnp.where(member, prompt_numbers[None, :], 0), axis=1)
    position = (row_index - first_row).astype(jnp.float32)
    return (member, position, prompt_start, prompt_index)


def rotate(values, position):
    half_width = values.shape[-1] // 2
    frequency = jnp.exp(
        jnp.arange(half_width, dtype=jnp.float32) * (-math.log(10000.0) / half_width)
    )
    angles = position[:, None, None] * frequency[None, None, :]
    cosine = jnp.cos(angles)
    sine = jnp.sin(angles)
    leading = values[..., :half_width]
    trailing = values[..., half_width:]
    return jnp.concatenate(
        [leading * cosine - trailing * sine, trailing * cosine + leading * sine], axis=-1
    )


def attend(queries, keys_rot, values, prompt_index):
    row_number_count = queries.shape[0]
    head_width = queries.shape[2]
    row_index = jnp.arange(row_number_count, dtype=jnp.int32)
    allowed = (prompt_index[:, None] == prompt_index[None, :]) & (
        row_index[None, :] <= row_index[:, None]
    )
    scores = jnp.einsum("thd,sd->hts", queries, keys_rot, preferred_element_type=jnp.float32) * (
        1.0 / math.sqrt(head_width)
    )
    scores = jnp.where(allowed[None, :, :], scores, -jnp.inf)
    row_peak = jnp.max(scores, axis=-1, keepdims=True)
    weights = jnp.exp(scores - row_peak)
    probs = (weights / jnp.sum(weights, axis=-1, keepdims=True)).astype(jnp.bfloat16)
    context = jnp.einsum("hts,sd->thd", probs, values, preferred_element_type=jnp.float32)
    return context.astype(jnp.bfloat16)


def fill_pages(kv_rot, lengths_row, prompt_start, table_row, page_slots):
    page_count = table_row.shape[0]
    prompt_count = lengths_row.shape[0]
    per_prompt = page_count // prompt_count
    page_index = jnp.arange(page_count, dtype=jnp.int32)
    entry = jnp.sum(
        jnp.where(table_row[None, :] == page_index[:, None], page_index[None, :], 0), axis=1
    )
    prompt_of = entry // per_prompt
    page_of = entry % per_prompt
    prompt_numbers = jnp.arange(prompt_count, dtype=jnp.int32)
    chosen = prompt_of[:, None] == prompt_numbers[None, :]
    prompt_len = jnp.sum(jnp.where(chosen, lengths_row[None, :], 0), axis=1)
    base_row = jnp.sum(jnp.where(chosen, prompt_start[None, :], 0), axis=1)
    within = page_of[:, None] * page_slots + jnp.arange(page_slots, dtype=jnp.int32)[None, :]
    valid = within < prompt_len[:, None]
    source = jnp.minimum(base_row[:, None] + within, kv_rot.shape[0] - 1)
    return jnp.where(valid[:, :, None], kv_rot[source], jnp.zeros((), kv_rot.dtype))


def swap(x, axis_name):
    return lax.ppermute(x, axis_name, [(0, 1), (1, 0)])


def pair_join(own, other, own_slot, axis):
    first = own_slot == 0
    lower = jnp.where(first, own, other)
    upper = jnp.where(first, other, own)
    return jnp.concatenate([lower, upper], axis=axis)


def mp_gather(x, axis, mp_count):
    if mp_count == 2:
        return pair_join(x, swap(x, "mp"), lax.axis_index("mp"), axis)
    return lax.all_gather(x, "mp", axis=axis, tiled=True)


def mp_pieces(x, mp_count):
    if mp_count == 2:
        other = swap(x, "mp")
        first = lax.axis_index("mp") == 0
        return [jnp.where(first, x, other), jnp.where(first, other, x)]
    stacked = lax.all_gather(x, "mp", axis=0, tiled=False)
    return [stacked[m] for m in range(mp_count)]


def half_of(x, axis, which):
    width = x.shape[axis] // 2
    return lax.dynamic_slice_in_dim(x, which * width, width, axis)


def shards(
    tokens,
    layer_norm_gain,
    layer_norm_bias,
    query_weight,
    key_value_weight,
    output_weight,
    adapter_down_factors,
    adapter_up_factors,
    lengths,
    prompt_adapter,
    prompt_page_table,
    adapter_storage,
    mp_count,
):
    side = lax.axis_index("dl")
    mp_index = lax.axis_index("mp")
    own_rows = tokens.shape[0]
    group_count = lengths.shape[0]
    group_rows = own_rows // group_count
    prompt_count = lengths.shape[1]
    pair_rows = 2 * own_rows

    normed = layer_norm(tokens, layer_norm_gain, layer_norm_bias)

    shard_rows = query_weight.shape[0]
    rank_width = adapter_down_factors.shape[2]
    down_by_rank = jnp.swapaxes(adapter_down_factors, 1, 2)
    kv_share = key_value_weight
    if mp_count == 2:
        kv_share = half_of(key_value_weight, 1, mp_index)
    kept = (
        half_of(query_weight, 1, side),
        kv_share,
        down_by_rank,
        half_of(adapter_up_factors, 2, side),
    )
    sent = (
        half_of(query_weight, 1, 1 - side),
        kv_share,
        down_by_rank,
        half_of(adapter_up_factors, 2, 1 - side),
    )
    padded_rows = -(-shard_rows // 16) * 16
    kept_cols = [pack_columns(part, shard_rows, padded_rows) for part in kept]
    widths = [part.shape[1] for part in kept_cols]
    kept_block = jnp.concatenate(kept_cols, axis=1)
    sent_block = jnp.concatenate(
        [pack_columns(part, shard_rows, padded_rows) for part in sent], axis=1
    )
    pair_block = pair_join(kept_block[None], swap(sent_block, "dl")[None], side, 0)
    gathered = lax.all_gather(pair_block, "dh", axis=0, tiled=False)
    gathered = row_major(gathered).reshape((-1,) + gathered.shape[2:])
    shard_count = gathered.shape[0]
    offsets = [sum(widths[:i]) for i in range(len(widths))]
    unpacked = [
        unpack_columns(gathered[:, :, off : off + width], part.shape, shard_rows)
        for off, width, part in zip(offsets, widths, kept)
    ]
    _, _, down_all, up_cols = unpacked
    projection_block = gathered.reshape(-1, gathered.shape[2])

    out_kept = half_of(output_weight, 1, side)
    out_sent = half_of(output_weight, 1, 1 - side)
    out_pair = pair_join(out_kept[None], swap(out_sent, "dl")[None], side, 0)
    out_gathered = lax.all_gather(out_pair, "dh", axis=0, tiled=False)
    heads_per_block = out_gathered.shape[0] * out_gathered.shape[1] // (2 * mp_count)

    normed_padded = pad_features(normed, shard_count, padded_rows)
    row_half = own_rows // mp_count
    partner_piece = swap(
        lax.dynamic_slice_in_dim(normed_padded, mp_index * row_half, row_half, 0), "dl"
    )
    partner_normed = jnp.concatenate(mp_pieces(partner_piece, mp_count), axis=0)
    normed_pair = jnp.concatenate([normed_padded, partner_normed], axis=0)
    small = jnp.concatenate([lengths, prompt_adapter], axis=1)
    small_pair = jnp.concatenate([small, swap(small, "dl")], axis=0)
    lengths_pair = small_pair[:, :prompt_count]
    adapter_pair = small_pair[:, prompt_count:]

    member_grouped, position_grouped, start_grouped, index_grouped = jax.vmap(
        lambda one_row: layout(one_row, group_rows)
    )(lengths_pair)
    pair_groups = 2 * group_count
    pair_prompts = pair_groups * prompt_count
    own_prompts = group_count * prompt_count
    position = position_grouped.reshape(pair_rows)
    prompt_global = (
        index_grouped + (jnp.arange(pair_groups, dtype=jnp.int32) * prompt_count)[:, None]
    ).reshape(pair_rows)
    member = prompt_global[:, None] == jnp.arange(pair_prompts, dtype=jnp.int32)[None, :]

    adapter_count = adapter_storage.shape[0]
    adapter_numbers = jnp.arange(adapter_count, dtype=jnp.int32)
    adapters_flat = adapter_pair.reshape(pair_prompts)
    storage_slots = jnp.sum(
        jnp.where(adapter_numbers[None, :] == adapters_flat[:, None], adapter_storage[None, :], 0),
        axis=1,
    )
    slot_rows = down_all.shape[0]
    matches = (storage_slots[:, None] == jnp.arange(slot_rows, dtype=jnp.int32)[None, :]).astype(
        jnp.bfloat16
    )
    down_selected = jnp.einsum(
        "pn,nrd->prd", matches[:own_prompts], down_all, preferred_element_type=jnp.float32
    ).astype(jnp.bfloat16)
    up_selected = jnp.einsum(
        "pn,nrc->prc", matches, up_cols, preferred_element_type=jnp.float32
    ).astype(jnp.bfloat16)

    feature_columns = adapter_down_factors.shape[1]
    features = lax.dynamic_slice_in_dim(normed, mp_index * feature_columns, feature_columns, 1)
    own_member = member[:own_rows, :own_prompts]
    all_ranks = jnp.einsum(
        "tf,qf->tq",
        features,
        down_selected.reshape(own_prompts * rank_width, feature_columns),
        preferred_element_type=jnp.float32,
    ).reshape(own_rows, own_prompts, rank_width)
    rank_portion = jnp.sum(jnp.where(own_member[:, :, None], all_ranks, 0.0), axis=1)
    ranks = lax.psum(rank_portion, "mp").astype(jnp.bfloat16)
    ranks_pair = jnp.concatenate([ranks, swap(ranks, "dl")], axis=0)
    spread = jnp.where(member[:, :, None], ranks_pair[:, None, :], jnp.zeros((), jnp.bfloat16))
    adapted_queries = jnp.dot(
        spread.reshape(pair_rows, pair_prompts * rank_width),
        up_selected.reshape(pair_prompts * rank_width, -1),
        preferred_element_type=jnp.float32,
    )

    projected = jnp.dot(normed_pair, projection_block, preferred_element_type=jnp.float32)
    query_base = projected[:, : widths[0]]
    kv_base = projected[:, widths[0] : widths[0] + widths[1]]
    if mp_count == 2:
        kv_base = pair_join(kv_base, swap(kv_base, "mp"), mp_index, 1)
    queries = rotate(
        (query_base + adapted_queries).reshape(pair_rows, -1, HEAD_SIZE), position
    ).astype(jnp.bfloat16)
    keys_rot = rotate(kv_base[:, None, :HEAD_SIZE], position)[:, 0, :]
    kv_rot = jnp.concatenate([keys_rot, kv_base[:, HEAD_SIZE:]], axis=1).astype(jnp.bfloat16)
    local_heads = queries.shape[1]
    queries_grouped = queries.reshape(pair_groups, group_rows, local_heads, HEAD_SIZE)
    kv_grouped = kv_rot.reshape(pair_groups, group_rows, 2 * HEAD_SIZE)
    context_grouped = jax.vmap(
        lambda q_part, kv_part, idx_part: attend(
            q_part, kv_part[:, :HEAD_SIZE], kv_part[:, HEAD_SIZE:], idx_part
        )
    )(queries_grouped, kv_grouped, index_grouped)
    context = context_grouped.reshape(pair_rows, local_heads * HEAD_SIZE)

    partner_context = swap(context, "dl")
    partner_context = jnp.concatenate(
        [partner_context[own_rows:], partner_context[:own_rows]], axis=0
    )
    block = context.shape[1]
    if mp_count == 2:
        other_mp = 1 - mp_index
        pieces = [
            (context, 2 * mp_index + side),
            (swap(context, "mp"), 2 * other_mp + side),
            (partner_context, 2 * mp_index + 1 - side),
            (swap(partner_context, "mp"), 2 * other_mp + 1 - side),
        ]
    else:
        stacked = lax.all_gather(jnp.stack([context, partner_context]), "mp", axis=0, tiled=False)
        pieces = [
            (stacked[m, which], 2 * m + jnp.where(which == 0, side, 1 - side))
            for which in range(2)
            for m in range(mp_count)
        ]

    def project(row_start):
        total = None
        for piece, quarter in pieces:
            rows = lax.dynamic_slice_in_dim(out_gathered, quarter * (heads_per_block // 2), heads_per_block // 2, 0)
            part = jnp.einsum(
                "tabk,abkn->tn",
                piece[row_start : row_start + own_rows].reshape((own_rows,) + rows.shape[:3]),
                rows,
                preferred_element_type=jnp.float32,
            )
            total = part if total is None else total + part
        return total.astype(jnp.bfloat16)

    received_out = swap(project(own_rows), "dl")
    own_out = project(0)
    attn_proj = pair_join(own_out, received_out, side, 1)

    cache_grouped = jax.vmap(
        lambda kv_part, len_part, start_part, table_part: fill_pages(
            kv_part, len_part, start_part, table_part, PAGE
        )
    )(kv_grouped[:group_count], lengths, start_grouped[:group_count], prompt_page_table)
    kv_cache = cache_grouped.reshape(group_count * prompt_page_table.shape[1], PAGE, 2 * HEAD_SIZE)
    return (attn_proj, kv_cache)


def solution(mesh):
    dp_count = mesh.shape["dp"]
    mp_count = mesh.shape["mp"]
    pair_mesh = Mesh(
        mesh.devices.reshape(dp_count // 2, 2, mp_count), ("dh", "dl", "mp")
    )
    dp = ("dh", "dl")
    return jax.shard_map(
        functools.partial(shards, mp_count=mp_count),
        mesh=pair_mesh,
        in_specs=(
            P(dp, None),
            P(),
            P(),
            P(dp, "mp"),
            P(dp, None),
            P(dp, "mp"),
            P(dp, "mp", None),
            P(dp, None, "mp"),
            P(dp, None),
            P(dp, None),
            P(dp, None),
            P(),
        ),
        out_specs=(P(dp, "mp"), P(dp, None, None)),
        check_vma=False,
    )
```

```python
import functools
import math

import jax
import jax.numpy as jnp
from jax import lax
from jax.sharding import Mesh, PartitionSpec as P
from jax.experimental.layout import Layout, with_layout_constraint

HEAD_SIZE = 64
PAGE = 128


def pack_columns(part, shard_rows, padded_rows):
    flat = part.reshape(-1)
    width = -(-flat.shape[0] // shard_rows)
    flat = jnp.pad(flat, (0, width * shard_rows - flat.shape[0]))
    return jnp.pad(flat.reshape(shard_rows, width), ((0, padded_rows - shard_rows), (0, 0)))


def unpack_columns(block, shape, shard_rows):
    shard_count = block.shape[0]
    size = math.prod(shape)
    flat = block[:, :shard_rows, :].reshape(shard_count, -1)[:, :size]
    return flat.reshape((shard_count * shape[0],) + tuple(shape[1:]))


def pad_features(x, shard_count, padded_rows):
    rows, width = x.shape
    split = x.reshape(rows, shard_count, width // shard_count)
    split = jnp.pad(split, ((0, 0), (0, 0), (0, padded_rows - width // shard_count)))
    return split.reshape(rows, shard_count * padded_rows)


def row_major(x):
    return with_layout_constraint(x, Layout(major_to_minor=tuple(range(x.ndim))))


def layer_norm(tokens, layer_norm_gain, layer_norm_bias):
    values = tokens.astype(jnp.float32)
    row_mean = jnp.mean(values, axis=-1, keepdims=True)
    centred = values - row_mean
    row_var = jnp.mean(centred * centred, axis=-1, keepdims=True)
    scaled = centred * lax.rsqrt(row_var + 1e-05)
    return (
        scaled * layer_norm_gain.astype(jnp.float32) + layer_norm_bias.astype(jnp.float32)
    ).astype(jnp.bfloat16)


def layout(lengths_row, row_number_count):
    prompt_end = jnp.cumsum(lengths_row)
    prompt_start = prompt_end - lengths_row
    row_index = jnp.arange(row_number_count, dtype=jnp.int32)
    member = (row_index[:, None] >= prompt_start[None, :]) & (
        row_index[:, None] < prompt_end[None, :]
    )
    first_row = jnp.sum(jnp.where(member, prompt_start[None, :], 0), axis=1)
    prompt_numbers = jnp.arange(lengths_row.shape[0], dtype=jnp.int32)
    prompt_index = jnp.sum(jnp.where(member, prompt_numbers[None, :], 0), axis=1)
    position = (row_index - first_row).astype(jnp.float32)
    return (member, position, prompt_start, prompt_index)


def rotate(values, position):
    half_width = values.shape[-1] // 2
    frequency = jnp.exp(
        jnp.arange(half_width, dtype=jnp.float32) * (-math.log(10000.0) / half_width)
    )
    angles = position[:, None, None] * frequency[None, None, :]
    cosine = jnp.cos(angles)
    sine = jnp.sin(angles)
    leading = values[..., :half_width]
    trailing = values[..., half_width:]
    return jnp.concatenate(
        [leading * cosine - trailing * sine, trailing * cosine + leading * sine], axis=-1
    )


def attend(queries, keys_rot, values, prompt_index):
    row_number_count = queries.shape[0]
    head_width = queries.shape[2]
    row_index = jnp.arange(row_number_count, dtype=jnp.int32)
    allowed = (prompt_index[:, None] == prompt_index[None, :]) & (
        row_index[None, :] <= row_index[:, None]
    )
    scores = jnp.einsum("thd,sd->hts", queries, keys_rot, preferred_element_type=jnp.float32) * (
        1.0 / math.sqrt(head_width)
    )
    scores = jnp.where(allowed[None, :, :], scores, -jnp.inf)
    row_peak = jnp.max(scores, axis=-1, keepdims=True)
    weights = jnp.exp(scores - row_peak)
    probs = (weights / jnp.sum(weights, axis=-1, keepdims=True)).astype(jnp.bfloat16)
    context = jnp.einsum("hts,sd->thd", probs, values, preferred_element_type=jnp.float32)
    return context.astype(jnp.bfloat16)


def fill_pages(kv_rot, lengths_row, prompt_start, table_row, page_slots):
    page_count = table_row.shape[0]
    prompt_count = lengths_row.shape[0]
    per_prompt = page_count // prompt_count
    page_index = jnp.arange(page_count, dtype=jnp.int32)
    entry = jnp.sum(
        jnp.where(table_row[None, :] == page_index[:, None], page_index[None, :], 0), axis=1
    )
    prompt_of = entry // per_prompt
    page_of = entry % per_prompt
    prompt_numbers = jnp.arange(prompt_count, dtype=jnp.int32)
    chosen = prompt_of[:, None] == prompt_numbers[None, :]
    prompt_len = jnp.sum(jnp.where(chosen, lengths_row[None, :], 0), axis=1)
    base_row = jnp.sum(jnp.where(chosen, prompt_start[None, :], 0), axis=1)
    within = page_of[:, None] * page_slots + jnp.arange(page_slots, dtype=jnp.int32)[None, :]
    valid = within < prompt_len[:, None]
    source = jnp.minimum(base_row[:, None] + within, kv_rot.shape[0] - 1)
    return jnp.where(valid[:, :, None], kv_rot[source], jnp.zeros((), kv_rot.dtype))


def swap(x, axis_name):
    return lax.ppermute(x, axis_name, [(0, 1), (1, 0)])


def pair_join(own, other, own_slot, axis):
    first = own_slot == 0
    lower = jnp.where(first, own, other)
    upper = jnp.where(first, other, own)
    return jnp.concatenate([lower, upper], axis=axis)


def mp_gather(x, axis, mp_count):
    if mp_count == 2:
        return pair_join(x, swap(x, "mp"), lax.axis_index("mp"), axis)
    return lax.all_gather(x, "mp", axis=axis, tiled=True)


def mp_pieces(x, mp_count):
    if mp_count == 2:
        other = swap(x, "mp")
        first = lax.axis_index("mp") == 0
        return [jnp.where(first, x, other), jnp.where(first, other, x)]
    stacked = lax.all_gather(x, "mp", axis=0, tiled=False)
    return [stacked[m] for m in range(mp_count)]


def gather_by_permutes(x, axis_name, count):
    by_shift = [x] + [
        lax.ppermute(x, axis_name, [(i, (i + shift) % count) for i in range(count)])
        for shift in range(1, count)
    ]
    reverse = jnp.stack(by_shift[::-1])
    doubled = jnp.concatenate([reverse, reverse], axis=0)
    start = (count - 1 - lax.axis_index(axis_name)) % count
    return lax.dynamic_slice_in_dim(doubled, start, count, 0)


def half_of(x, axis, which):
    width = x.shape[axis] // 2
    return lax.dynamic_slice_in_dim(x, which * width, width, axis)


def shards(
    tokens,
    layer_norm_gain,
    layer_norm_bias,
    query_weight,
    key_value_weight,
    output_weight,
    adapter_down_factors,
    adapter_up_factors,
    lengths,
    prompt_adapter,
    prompt_page_table,
    adapter_storage,
    mp_count,
    dh_count,
):
    side = lax.axis_index("dl")
    mp_index = lax.axis_index("mp")
    own_rows = tokens.shape[0]
    group_count = lengths.shape[0]
    group_rows = own_rows // group_count
    prompt_count = lengths.shape[1]
    pair_rows = 2 * own_rows

    normed = layer_norm(tokens, layer_norm_gain, layer_norm_bias)

    shard_rows = query_weight.shape[0]
    rank_width = adapter_down_factors.shape[2]
    down_by_rank = jnp.swapaxes(adapter_down_factors, 1, 2)
    kept = (
        half_of(query_weight, 1, side),
        key_value_weight,
        down_by_rank,
        half_of(adapter_up_factors, 2, side),
    )
    sent = (
        half_of(query_weight, 1, 1 - side),
        key_value_weight,
        down_by_rank,
        half_of(adapter_up_factors, 2, 1 - side),
    )
    padded_rows = -(-shard_rows // 16) * 16
    kept_cols = [pack_columns(part, shard_rows, padded_rows) for part in kept]
    widths = [part.shape[1] for part in kept_cols]
    kept_block = jnp.concatenate(kept_cols, axis=1)
    sent_block = jnp.concatenate(
        [pack_columns(part, shard_rows, padded_rows) for part in sent], axis=1
    )
    pair_block = pair_join(kept_block[None], swap(sent_block, "dl")[None], side, 0)
    gathered = lax.all_gather(pair_block, "dh", axis=0, tiled=False)
    gathered = row_major(gathered).reshape((-1,) + gathered.shape[2:])
    shard_count = gathered.shape[0]
    offsets = [sum(widths[:i]) for i in range(len(widths))]
    unpacked = [
        unpack_columns(gathered[:, :, off : off + width], part.shape, shard_rows)
        for off, width, part in zip(offsets, widths, kept)
    ]
    _, _, down_all, up_cols = unpacked
    projection_block = gathered.reshape(-1, gathered.shape[2])

    out_kept = half_of(output_weight, 1, side)
    out_sent = half_of(output_weight, 1, 1 - side)
    out_pair = pair_join(out_kept[None], swap(out_sent, "dl")[None], side, 0)
    out_gathered = gather_by_permutes(out_pair, "dh", dh_count)
    heads_per_block = out_gathered.shape[0] * out_gathered.shape[1] // (2 * mp_count)

    normed_padded = pad_features(normed, shard_count, padded_rows)
    row_half = own_rows // mp_count
    partner_piece = swap(
        lax.dynamic_slice_in_dim(normed_padded, mp_index * row_half, row_half, 0), "dl"
    )
    partner_normed = jnp.concatenate(mp_pieces(partner_piece, mp_count), axis=0)
    normed_pair = jnp.concatenate([normed_padded, partner_normed], axis=0)
    small = jnp.concatenate([lengths, prompt_adapter], axis=1)
    small_pair = jnp.concatenate([small, swap(small, "dl")], axis=0)
    lengths_pair = small_pair[:, :prompt_count]
    adapter_pair = small_pair[:, prompt_count:]

    member_grouped, position_grouped, start_grouped, index_grouped = jax.vmap(
        lambda one_row: layout(one_row, group_rows)
    )(lengths_pair)
    pair_groups = 2 * group_count
    pair_prompts = pair_groups * prompt_count
    own_prompts = group_count * prompt_count
    position = position_grouped.reshape(pair_rows)
    prompt_global = (
        index_grouped + (jnp.arange(pair_groups, dtype=jnp.int32) * prompt_count)[:, None]
    ).reshape(pair_rows)
    member = prompt_global[:, None] == jnp.arange(pair_prompts, dtype=jnp.int32)[None, :]

    adapter_count = adapter_storage.shape[0]
    adapter_numbers = jnp.arange(adapter_count, dtype=jnp.int32)
    adapters_flat = adapter_pair.reshape(pair_prompts)
    storage_slots = jnp.sum(
        jnp.where(adapter_numbers[None, :] == adapters_flat[:, None], adapter_storage[None, :], 0),
        axis=1,
    )
    slot_rows = down_all.shape[0]
    matches = (storage_slots[:, None] == jnp.arange(slot_rows, dtype=jnp.int32)[None, :]).astype(
        jnp.bfloat16
    )
    down_selected = jnp.einsum(
        "pn,nrd->prd", matches[:own_prompts], down_all, preferred_element_type=jnp.float32
    ).astype(jnp.bfloat16)
    up_selected = jnp.einsum(
        "pn,nrc->prc", matches, up_cols, preferred_element_type=jnp.float32
    ).astype(jnp.bfloat16)

    feature_columns = adapter_down_factors.shape[1]
    features = lax.dynamic_slice_in_dim(normed, mp_index * feature_columns, feature_columns, 1)
    own_member = member[:own_rows, :own_prompts]
    all_ranks = jnp.einsum(
        "tf,qf->tq",
        features,
        down_selected.reshape(own_prompts * rank_width, feature_columns),
        preferred_element_type=jnp.float32,
    ).reshape(own_rows, own_prompts, rank_width)
    rank_portion = jnp.sum(jnp.where(own_member[:, :, None], all_ranks, 0.0), axis=1)
    ranks = lax.psum(rank_portion, "mp").astype(jnp.bfloat16)
    ranks_pair = jnp.concatenate([ranks, swap(ranks, "dl")], axis=0)
    spread = jnp.where(member[:, :, None], ranks_pair[:, None, :], jnp.zeros((), jnp.bfloat16))
    adapted_queries = jnp.dot(
        spread.reshape(pair_rows, pair_prompts * rank_width),
        up_selected.reshape(pair_prompts * rank_width, -1),
        preferred_element_type=jnp.float32,
    )

    projected = jnp.dot(normed_pair, projection_block, preferred_element_type=jnp.float32)
    query_base = projected[:, : widths[0]]
    kv_base = projected[:, widths[0] : widths[0] + widths[1]]
    queries = rotate(
        (query_base + adapted_queries).reshape(pair_rows, -1, HEAD_SIZE), position
    ).astype(jnp.bfloat16)
    keys_rot = rotate(kv_base[:, None, :HEAD_SIZE], position)[:, 0, :]
    kv_rot = jnp.concatenate([keys_rot, kv_base[:, HEAD_SIZE:]], axis=1).astype(jnp.bfloat16)
    local_heads = queries.shape[1]
    queries_grouped = queries.reshape(pair_groups, group_rows, local_heads, HEAD_SIZE)
    kv_grouped = kv_rot.reshape(pair_groups, group_rows, 2 * HEAD_SIZE)
    context_grouped = jax.vmap(
        lambda q_part, kv_part, idx_part: attend(
            q_part, kv_part[:, :HEAD_SIZE], kv_part[:, HEAD_SIZE:], idx_part
        )
    )(queries_grouped, kv_grouped, index_grouped)
    context = context_grouped.reshape(pair_rows, local_heads * HEAD_SIZE)

    partner_context = swap(context, "dl")
    partner_context = jnp.concatenate(
        [partner_context[own_rows:], partner_context[:own_rows]], axis=0
    )
    block = context.shape[1]
    if mp_count == 2:
        other_mp = 1 - mp_index
        pieces = [
            (context, 2 * mp_index + side),
            (swap(context, "mp"), 2 * other_mp + side),
            (partner_context, 2 * mp_index + 1 - side),
            (swap(partner_context, "mp"), 2 * other_mp + 1 - side),
        ]
    else:
        stacked = lax.all_gather(jnp.stack([context, partner_context]), "mp", axis=0, tiled=False)
        pieces = [
            (stacked[m, which], 2 * m + jnp.where(which == 0, side, 1 - side))
            for which in range(2)
            for m in range(mp_count)
        ]

    def project(row_start):
        total = None
        for piece, quarter in pieces:
            rows = lax.dynamic_slice_in_dim(out_gathered, quarter * (heads_per_block // 2), heads_per_block // 2, 0)
            part = jnp.einsum(
                "tabk,abkn->tn",
                piece[row_start : row_start + own_rows].reshape((own_rows,) + rows.shape[:3]),
                rows,
                preferred_element_type=jnp.float32,
            )
            total = part if total is None else total + part
        return total.astype(jnp.bfloat16)

    received_out = swap(project(own_rows), "dl")
    own_out = project(0)
    attn_proj = pair_join(own_out, received_out, side, 1)

    cache_grouped = jax.vmap(
        lambda kv_part, len_part, start_part, table_part: fill_pages(
            kv_part, len_part, start_part, table_part, PAGE
        )
    )(kv_grouped[:group_count], lengths, start_grouped[:group_count], prompt_page_table)
    kv_cache = cache_grouped.reshape(group_count * prompt_page_table.shape[1], PAGE, 2 * HEAD_SIZE)
    return (attn_proj, kv_cache)


def solution(mesh):
    dp_count = mesh.shape["dp"]
    mp_count = mesh.shape["mp"]
    pair_mesh = Mesh(
        mesh.devices.reshape(dp_count // 2, 2, mp_count), ("dh", "dl", "mp")
    )
    dp = ("dh", "dl")
    return jax.shard_map(
        functools.partial(shards, mp_count=mp_count, dh_count=dp_count // 2),
        mesh=pair_mesh,
        in_specs=(
            P(dp, None),
            P(),
            P(),
            P(dp, "mp"),
            P(dp, None),
            P(dp, "mp"),
            P(dp, "mp", None),
            P(dp, None, "mp"),
            P(dp, None),
            P(dp, None),
            P(dp, None),
            P(),
        ),
        out_specs=(P(dp, "mp"), P(dp, None, None)),
        check_vma=False,
    )
```

```python
import functools
import math

import jax
import jax.numpy as jnp
from jax import lax
from jax.sharding import Mesh, PartitionSpec as P
from jax.experimental.layout import Layout, with_layout_constraint

HEAD_SIZE = 64
PAGE = 128


def pack_columns(part, shard_rows, padded_rows):
    flat = part.reshape(-1)
    width = -(-flat.shape[0] // shard_rows)
    flat = jnp.pad(flat, (0, width * shard_rows - flat.shape[0]))
    return jnp.pad(flat.reshape(shard_rows, width), ((0, padded_rows - shard_rows), (0, 0)))


def unpack_columns(block, shape, shard_rows):
    shard_count = block.shape[0]
    size = math.prod(shape)
    flat = block[:, :shard_rows, :].reshape(shard_count, -1)[:, :size]
    return flat.reshape((shard_count * shape[0],) + tuple(shape[1:]))


def pad_features(x, shard_count, padded_rows):
    rows, width = x.shape
    split = x.reshape(rows, shard_count, width // shard_count)
    split = jnp.pad(split, ((0, 0), (0, 0), (0, padded_rows - width // shard_count)))
    return split.reshape(rows, shard_count * padded_rows)


def row_major(x):
    return with_layout_constraint(x, Layout(major_to_minor=tuple(range(x.ndim))))


def layer_norm(tokens, layer_norm_gain, layer_norm_bias):
    values = tokens.astype(jnp.float32)
    row_mean = jnp.mean(values, axis=-1, keepdims=True)
    centred = values - row_mean
    row_var = jnp.mean(centred * centred, axis=-1, keepdims=True)
    scaled = centred * lax.rsqrt(row_var + 1e-05)
    return (
        scaled * layer_norm_gain.astype(jnp.float32) + layer_norm_bias.astype(jnp.float32)
    ).astype(jnp.bfloat16)


def layout(lengths_row, row_number_count):
    prompt_end = jnp.cumsum(lengths_row)
    prompt_start = prompt_end - lengths_row
    row_index = jnp.arange(row_number_count, dtype=jnp.int32)
    member = (row_index[:, None] >= prompt_start[None, :]) & (
        row_index[:, None] < prompt_end[None, :]
    )
    first_row = jnp.sum(jnp.where(member, prompt_start[None, :], 0), axis=1)
    prompt_numbers = jnp.arange(lengths_row.shape[0], dtype=jnp.int32)
    prompt_index = jnp.sum(jnp.where(member, prompt_numbers[None, :], 0), axis=1)
    position = (row_index - first_row).astype(jnp.float32)
    return (member, position, prompt_start, prompt_index)


def rotate(values, position):
    half_width = values.shape[-1] // 2
    frequency = jnp.exp(
        jnp.arange(half_width, dtype=jnp.float32) * (-math.log(10000.0) / half_width)
    )
    angles = position[:, None, None] * frequency[None, None, :]
    cosine = jnp.cos(angles)
    sine = jnp.sin(angles)
    leading = values[..., :half_width]
    trailing = values[..., half_width:]
    return jnp.concatenate(
        [leading * cosine - trailing * sine, trailing * cosine + leading * sine], axis=-1
    )


def attend(queries, keys_rot, values, prompt_index):
    row_number_count = queries.shape[0]
    head_width = queries.shape[2]
    row_index = jnp.arange(row_number_count, dtype=jnp.int32)
    allowed = (prompt_index[:, None] == prompt_index[None, :]) & (
        row_index[None, :] <= row_index[:, None]
    )
    scores = jnp.einsum("thd,sd->hts", queries, keys_rot, preferred_element_type=jnp.float32) * (
        1.0 / math.sqrt(head_width)
    )
    scores = jnp.where(allowed[None, :, :], scores, -jnp.inf)
    row_peak = jnp.max(scores, axis=-1, keepdims=True)
    weights = jnp.exp(scores - row_peak)
    probs = (weights / jnp.sum(weights, axis=-1, keepdims=True)).astype(jnp.bfloat16)
    context = jnp.einsum("hts,sd->thd", probs, values, preferred_element_type=jnp.float32)
    return context.astype(jnp.bfloat16)


def fill_pages(kv_rot, lengths_row, prompt_start, table_row, page_slots):
    page_count = table_row.shape[0]
    prompt_count = lengths_row.shape[0]
    per_prompt = page_count // prompt_count
    page_index = jnp.arange(page_count, dtype=jnp.int32)
    entry = jnp.sum(
        jnp.where(table_row[None, :] == page_index[:, None], page_index[None, :], 0), axis=1
    )
    prompt_of = entry // per_prompt
    page_of = entry % per_prompt
    prompt_numbers = jnp.arange(prompt_count, dtype=jnp.int32)
    chosen = prompt_of[:, None] == prompt_numbers[None, :]
    prompt_len = jnp.sum(jnp.where(chosen, lengths_row[None, :], 0), axis=1)
    base_row = jnp.sum(jnp.where(chosen, prompt_start[None, :], 0), axis=1)
    within = page_of[:, None] * page_slots + jnp.arange(page_slots, dtype=jnp.int32)[None, :]
    valid = within < prompt_len[:, None]
    source = jnp.minimum(base_row[:, None] + within, kv_rot.shape[0] - 1)
    return jnp.where(valid[:, :, None], kv_rot[source], jnp.zeros((), kv_rot.dtype))


def swap(x, axis_name):
    return lax.ppermute(x, axis_name, [(0, 1), (1, 0)])


def pair_join(own, other, own_slot, axis):
    first = own_slot == 0
    lower = jnp.where(first, own, other)
    upper = jnp.where(first, other, own)
    return jnp.concatenate([lower, upper], axis=axis)


def mp_gather(x, axis, mp_count):
    if mp_count == 2:
        return pair_join(x, swap(x, "mp"), lax.axis_index("mp"), axis)
    return lax.all_gather(x, "mp", axis=axis, tiled=True)


def mp_pieces(x, mp_count):
    if mp_count == 2:
        other = swap(x, "mp")
        first = lax.axis_index("mp") == 0
        return [jnp.where(first, x, other), jnp.where(first, other, x)]
    stacked = lax.all_gather(x, "mp", axis=0, tiled=False)
    return [stacked[m] for m in range(mp_count)]


def half_of(x, axis, which):
    width = x.shape[axis] // 2
    return lax.dynamic_slice_in_dim(x, which * width, width, axis)


def shards(
    tokens,
    layer_norm_gain,
    layer_norm_bias,
    query_weight,
    key_value_weight,
    output_weight,
    adapter_down_factors,
    adapter_up_factors,
    lengths,
    prompt_adapter,
    prompt_page_table,
    adapter_storage,
    mp_count,
):
    side = lax.axis_index("dl")
    mp_index = lax.axis_index("mp")
    own_rows = tokens.shape[0]
    group_count = lengths.shape[0]
    group_rows = own_rows // group_count
    prompt_count = lengths.shape[1]
    pair_rows = 2 * own_rows

    normed = layer_norm(tokens, layer_norm_gain, layer_norm_bias)

    shard_rows = query_weight.shape[0]
    rank_width = adapter_down_factors.shape[2]
    down_by_rank = jnp.swapaxes(adapter_down_factors, 1, 2)
    kept = (
        half_of(query_weight, 1, side),
        key_value_weight,
        down_by_rank,
        half_of(adapter_up_factors, 2, side),
    )
    sent = (
        half_of(query_weight, 1, 1 - side),
        key_value_weight,
        down_by_rank,
        half_of(adapter_up_factors, 2, 1 - side),
    )
    padded_rows = -(-shard_rows // 16) * 16
    kept_cols = [pack_columns(part, shard_rows, padded_rows) for part in kept]
    widths = [part.shape[1] for part in kept_cols]
    kept_block = jnp.concatenate(kept_cols, axis=1)
    sent_block = jnp.concatenate(
        [pack_columns(part, shard_rows, padded_rows) for part in sent], axis=1
    )
    pair_block = pair_join(kept_block[None], swap(sent_block, "dl")[None], side, 0)
    gathered = lax.all_gather(pair_block, "dh", axis=0, tiled=False)
    gathered = row_major(gathered).reshape((-1,) + gathered.shape[2:])
    shard_count = gathered.shape[0]
    offsets = [sum(widths[:i]) for i in range(len(widths))]
    unpacked = [
        unpack_columns(gathered[:, :, off : off + width], part.shape, shard_rows)
        for off, width, part in zip(offsets, widths, kept)
    ]
    _, _, down_all, up_cols = unpacked
    projection_block = gathered.reshape(-1, gathered.shape[2])

    out_kept = half_of(output_weight, 1, side)
    out_sent = half_of(output_weight, 1, 1 - side)
    out_pair = pair_join(out_kept[None], swap(out_sent, "dl")[None], side, 0)
    out_gathered = lax.all_gather(out_pair, "dh", axis=0, tiled=False)
    heads_per_block = out_gathered.shape[0] * out_gathered.shape[1] // (2 * mp_count)

    normed_padded = pad_features(normed, shard_count, padded_rows)
    row_half = own_rows // mp_count
    partner_piece = swap(
        lax.dynamic_slice_in_dim(normed_padded, mp_index * row_half, row_half, 0), "dl"
    )
    partner_normed = jnp.concatenate(mp_pieces(partner_piece, mp_count), axis=0)
    normed_pair = jnp.concatenate([normed_padded, partner_normed], axis=0)
    small = jnp.concatenate([lengths, prompt_adapter], axis=1)
    small_pair = jnp.concatenate([small, swap(small, "dl")], axis=0)
    lengths_pair = small_pair[:, :prompt_count]
    adapter_pair = small_pair[:, prompt_count:]

    member_grouped, position_grouped, start_grouped, index_grouped = jax.vmap(
        lambda one_row: layout(one_row, group_rows)
    )(lengths_pair)
    pair_groups = 2 * group_count
    pair_prompts = pair_groups * prompt_count
    own_prompts = group_count * prompt_count
    position = position_grouped.reshape(pair_rows)
    prompt_global = (
        index_grouped + (jnp.arange(pair_groups, dtype=jnp.int32) * prompt_count)[:, None]
    ).reshape(pair_rows)
    member = prompt_global[:, None] == jnp.arange(pair_prompts, dtype=jnp.int32)[None, :]

    adapter_count = adapter_storage.shape[0]
    adapter_numbers = jnp.arange(adapter_count, dtype=jnp.int32)
    adapters_flat = adapter_pair.reshape(pair_prompts)
    storage_slots = jnp.sum(
        jnp.where(adapter_numbers[None, :] == adapters_flat[:, None], adapter_storage[None, :], 0),
        axis=1,
    )
    slot_rows = down_all.shape[0]
    matches = (storage_slots[:, None] == jnp.arange(slot_rows, dtype=jnp.int32)[None, :]).astype(
        jnp.bfloat16
    )
    down_selected = jnp.einsum(
        "pn,nrd->prd", matches[:own_prompts], down_all, preferred_element_type=jnp.float32
    ).astype(jnp.bfloat16)
    up_selected = jnp.einsum(
        "pn,nrc->prc", matches, up_cols, preferred_element_type=jnp.float32
    ).astype(jnp.bfloat16)

    feature_columns = adapter_down_factors.shape[1]
    features = lax.dynamic_slice_in_dim(normed, mp_index * feature_columns, feature_columns, 1)
    own_member = member[:own_rows, :own_prompts]
    all_ranks = jnp.einsum(
        "tf,qf->tq",
        features,
        down_selected.reshape(own_prompts * rank_width, feature_columns),
        preferred_element_type=jnp.float32,
    ).reshape(own_rows, own_prompts, rank_width)
    rank_portion = jnp.sum(jnp.where(own_member[:, :, None], all_ranks, 0.0), axis=1)
    ranks = lax.psum(rank_portion, "mp").astype(jnp.bfloat16)
    ranks_pair = jnp.concatenate([ranks, swap(ranks, "dl")], axis=0)
    spread = jnp.where(member[:, :, None], ranks_pair[:, None, :], jnp.zeros((), jnp.bfloat16))
    adapted_queries = jnp.dot(
        spread.reshape(pair_rows, pair_prompts * rank_width),
        up_selected.reshape(pair_prompts * rank_width, -1),
        preferred_element_type=jnp.float32,
    )

    projected = jnp.dot(normed_pair, projection_block, preferred_element_type=jnp.float32)
    query_base = projected[:, : widths[0]]
    kv_base = projected[:, widths[0] : widths[0] + widths[1]]
    queries = rotate(
        (query_base + adapted_queries).reshape(pair_rows, -1, HEAD_SIZE), position
    ).astype(jnp.bfloat16)
    keys_rot = rotate(kv_base[:, None, :HEAD_SIZE], position)[:, 0, :]
    kv_rot = jnp.concatenate([keys_rot, kv_base[:, HEAD_SIZE:]], axis=1).astype(jnp.bfloat16)
    local_heads = queries.shape[1]
    queries_grouped = queries.reshape(pair_groups, group_rows, local_heads, HEAD_SIZE)
    kv_grouped = kv_rot.reshape(pair_groups, group_rows, 2 * HEAD_SIZE)
    context_grouped = jax.vmap(
        lambda q_part, kv_part, idx_part: attend(
            q_part, kv_part[:, :HEAD_SIZE], kv_part[:, HEAD_SIZE:], idx_part
        )
    )(queries_grouped, kv_grouped, index_grouped)
    context = context_grouped.reshape(pair_rows, local_heads * HEAD_SIZE)

    partner_context = swap(context, "dl")
    partner_context = jnp.concatenate(
        [partner_context[own_rows:], partner_context[:own_rows]], axis=0
    )
    block = context.shape[1]
    if mp_count == 2:
        other_mp = 1 - mp_index
        pieces = [
            (context, 2 * mp_index + side),
            (swap(context, "mp"), 2 * other_mp + side),
            (partner_context, 2 * mp_index + 1 - side),
            (swap(partner_context, "mp"), 2 * other_mp + 1 - side),
        ]
    else:
        stacked = lax.all_gather(jnp.stack([context, partner_context]), "mp", axis=0, tiled=False)
        pieces = [
            (stacked[m, which], 2 * m + jnp.where(which == 0, side, 1 - side))
            for which in range(2)
            for m in range(mp_count)
        ]

    def project(row_start, row_count=own_rows):
        total = None
        for piece, quarter in pieces:
            rows = lax.dynamic_slice_in_dim(out_gathered, quarter * (heads_per_block // 2), heads_per_block // 2, 0)
            part = jnp.einsum(
                "tabk,abkn->tn",
                piece[row_start : row_start + row_count].reshape((row_count,) + rows.shape[:3]),
                rows,
                preferred_element_type=jnp.float32,
            )
            total = part if total is None else total + part
        return total.astype(jnp.bfloat16)

    half_rows = own_rows // 2
    received_out = jnp.concatenate(
        [swap(project(own_rows, half_rows), "dl"), swap(project(own_rows + half_rows, half_rows), "dl")],
        axis=0,
    )
    own_out = project(0)
    attn_proj = pair_join(own_out, received_out, side, 1)

    cache_grouped = jax.vmap(
        lambda kv_part, len_part, start_part, table_part: fill_pages(
            kv_part, len_part, start_part, table_part, PAGE
        )
    )(kv_grouped[:group_count], lengths, start_grouped[:group_count], prompt_page_table)
    kv_cache = cache_grouped.reshape(group_count * prompt_page_table.shape[1], PAGE, 2 * HEAD_SIZE)
    return (attn_proj, kv_cache)


def solution(mesh):
    dp_count = mesh.shape["dp"]
    mp_count = mesh.shape["mp"]
    pair_mesh = Mesh(
        mesh.devices.reshape(dp_count // 2, 2, mp_count), ("dh", "dl", "mp")
    )
    dp = ("dh", "dl")
    return jax.shard_map(
        functools.partial(shards, mp_count=mp_count),
        mesh=pair_mesh,
        in_specs=(
            P(dp, None),
            P(),
            P(),
            P(dp, "mp"),
            P(dp, None),
            P(dp, "mp"),
            P(dp, "mp", None),
            P(dp, None, "mp"),
            P(dp, None),
            P(dp, None),
            P(dp, None),
            P(),
        ),
        out_specs=(P(dp, "mp"), P(dp, None, None)),
        check_vma=False,
    )
```
